32 devices in a mesh: section: 4 (over x, core), sp: 2 (over y), rep: 4 (over z).
Axes of the slice: x: 2, y: 2, z: 4, core: 2. Of those that a mesh axis runs over, the one named last changes fastest.
Arguments:
- tokens: float32 [2, 2, 24, 3072], P('sp', None, 'section', 'rep'), may hold values from -120 to 120
- mod_scale: float32 [3072], replicated, may hold values from -3 to 3
- mod_shift: float32 [3072], replicated, may hold values from -3 to 3
- proj_weight: float32 [64, 3072], replicated, may hold values from -0.109375 to 0.109375
- proj_bias: float32 [64], replicated, may hold values from -3 to 3
- noisy_latent: float32 [2, 4, 48, 16], P(None, 'sp', 'section'), may hold values from -120 to 120
- in_weight: float32 [3, 3, 3, 16, 512], replicated, may hold values from -0.3125 to 0.3125
- in_bias: float32 [512], replicated, may hold values from -3 to 3
- conv_weight: bfloat16 [3, 3, 3, 256, 512], P(None, None, None, 'rep'), may hold values from -0.0546875 to 0.0546875
- conv_bias: float32 [256], P('rep'), may hold values from -3 to 3
- norm_gain: float32 [256], P('rep'), may hold values from 0.25 to 1.75
- norm_bias: float32 [256], P('rep'), may hold values from -3 to 3
Outputs:
- decoded: float32 [8, 96, 512], P('sp', 'section', 'rep')
The draws below stay inside these ranges and needn't reach their ends.
All inputs are finite; a program needn't handle non-finite values.
Results may differ from the reference program's by a relative error of at most 0.0026.
Values sent between devices are 32-bit elements; how exact they have to be, the bound alone decides.
No kernel may reach another device: no remote copies, remote signals or barrier semaphores. Data moves between devices by JAX's collectives and lax.ppermute only.
A program may use at most 64 MiB of HBM per device.

```python
import math
import jax
import jax.numpy as jnp
from jax import lax

D = 3072
LC = 16
CM = 512
CO = 256
GROUPS = 32
LF = 2
HP = 2
WP = 24
LH = 4
LW = 48


def draw_tokens(key, part):
    subkeys = jax.random.split(key, 6)
    column_scale = 0.3 * jnp.power(10.0, jnp.arange(D, dtype=jnp.float32) / D) * jnp.exp(jax.random.uniform(subkeys[1], (D,), jnp.float32, -0.35, 0.35))
    row_scale = jnp.exp(jax.random.uniform(subkeys[2], (LF, HP, WP, 1), jnp.float32, -0.7, 0.7))
    common_vector = jnp.clip(jax.random.normal(subkeys[3], (D,), jnp.float32), -2.5, 2.5)
    half_octave = 0.5 * math.log(2.0)
    common_weight = 0.8 * jnp.exp(jax.random.uniform(subkeys[4], (LF, HP, 1, 1), jnp.float32, 0.0, half_octave) + jax.random.uniform(subkeys[5], (1, 1, WP, 1), jnp.float32, 0.0, half_octave))
    rough_part = jnp.clip(jax.random.normal(subkeys[0], (LF, HP, WP, D), jnp.float32), -3.5, 3.5)
    return (rough_part + common_weight * common_vector) * column_scale * row_scale


def draw_noisy_latent(key, part):
    subkeys = jax.random.split(key, 3)
    row_rise = jnp.power(3.0, jnp.arange(LH, dtype=jnp.float32) / (LH - 1)).reshape(1, LH, 1, 1)
    row_scale = row_rise * jnp.exp(jax.random.uniform(subkeys[1], (1, LH, 1, 1), jnp.float32, 0.0, math.log(3.3)))
    column_scale = jnp.exp(jax.random.uniform(subkeys[2], (1, 1, LW, 1), jnp.float32, 0.0, math.log(3.0)))
    normal_part = jnp.clip(jax.random.normal(subkeys[0], (LF, LH, LW, LC), jnp.float32), -4.0, 4.0)
    return 0.1 * normal_part * row_scale * column_scale


def block_levels(key, extent, pieces, least, largest):
    loudness, own = 1.0, jax.random.fold_in(key, 6)
    for dim, parts in pieces:
        draws = jnp.exp(jax.random.uniform(jax.random.fold_in(own, dim), (parts,), jnp.float32, least / len(pieces), largest / len(pieces)))
        loudness = loudness * jnp.repeat(draws, extent[dim] // parts).reshape([-1 if axis == dim else 1 for axis in range(len(extent))])
    return loudness


def noise(key, dims, scale, bound, shards=(), kind=jnp.bfloat16):
    entries = scale * jax.random.normal(key, dims, jnp.float32)
    if shards:
        entries = entries * block_levels(key, dims, shards, -0.22, 0.18)
    return jnp.clip(entries, -bound, bound).astype(kind)


def setup_inputs(seed: int = 0) -> dict:
    splits = jax.random.split(jax.random.key(seed), 13)
    tokens = draw_tokens(jax.random.fold_in(splits[12], 71), 0)
    mod_scale = noise(splits[1], (D,), 0.3, 3.0, (), jnp.float32)
    mod_shift = noise(splits[2], (D,), 0.5, 3.0, (), jnp.float32)
    proj_weight = noise(splits[3], (4 * LC, D), D ** -0.5, 0.109375, (), jnp.float32)
    proj_bias = noise(splits[4], (4 * LC,), 0.5, 3.0, (), jnp.float32)
    noisy_latent = draw_noisy_latent(jax.random.fold_in(splits[12], 71), 0)
    in_weight = noise(splits[6], (3, 3, 3, LC, CM), (27 * LC) ** -0.5, 0.3125, (), jnp.float32)
    in_bias = noise(splits[7], (CM,), 0.3, 3.0, (), jnp.float32)
    conv_weight = noise(splits[8], (3, 3, 3, CO, CM), (27 * CM) ** -0.5, 0.0546875, ((3, 4),))
    conv_bias = noise(splits[9], (CO,), 0.3, 3.0, ((0, 4),), jnp.float32)
    norm_gain = jnp.clip(1.0 + 0.15 * jax.random.normal(splits[10], (CO,), jnp.float32), 0.25, 1.75)
    norm_bias = noise(splits[11], (CO,), 0.5, 3.0, ((0, 4),), jnp.float32)
    return {"tokens": tokens, "mod_scale": mod_scale, "mod_shift": mod_shift, "proj_weight": proj_weight, "proj_bias": proj_bias, "noisy_latent": noisy_latent, "in_weight": in_weight, "in_bias": in_bias, "conv_weight": conv_weight, "conv_bias": conv_bias, "norm_gain": norm_gain, "norm_bias": norm_bias}


def causal_conv(volume, kernel, kernel_spec, precision_mode):
    front = jnp.concatenate([volume[:1], volume[:1], volume], axis=0)
    padded = jnp.pad(front, ((0, 0), (1, 1), (1, 1), (0, 0)))
    result = lax.conv_general_dilated(padded[None], kernel, (1, 1, 1), 'VALID', dimension_numbers=('NDHWC', kernel_spec, 'NDHWC'), precision=precision_mode, preferred_element_type=jnp.float32)
    return result[0]

def reference(tokens, mod_scale, mod_shift, proj_weight, proj_bias, noisy_latent, in_weight, in_bias, conv_weight, conv_bias, norm_gain, norm_bias):
    token_mean = lax.optimization_barrier(jnp.mean(tokens, axis=-1, keepdims=True))
    token_var = lax.optimization_barrier(jnp.mean(jnp.square(tokens - token_mean), axis=-1, keepdims=True))
    modulated = (tokens - token_mean) * lax.rsqrt(token_var + 1e-06) * (1.0 + mod_scale) + mod_shift
    velocity = lax.dot_general(modulated.reshape(-1, D), proj_weight, (((1,), (1,)), ((), ())), precision=lax.Precision.HIGHEST, preferred_element_type=jnp.float32) + proj_bias
    patches = velocity.reshape(LF, HP, WP, LC, 2, 2).transpose(0, 1, 4, 2, 5, 3).reshape(LF, LH, LW, LC)
    clean = noisy_latent - 0.5 * patches
    features = (causal_conv(clean, in_weight, 'DHWIO', lax.Precision.HIGHEST) + in_bias).astype(jnp.bfloat16)
    upsampled = jnp.repeat(jnp.repeat(features, 2, axis=1), 2, axis=2)
    mixed = causal_conv(upsampled, conv_weight, 'DHWOI', None) + conv_bias
    grouped = mixed.reshape(LF, 2 * LH, 2 * LW, GROUPS, CO // GROUPS)
    group_mean = lax.optimization_barrier(jnp.mean(grouped, axis=(0, 1, 2, 4), keepdims=True))
    group_var = lax.optimization_barrier(jnp.mean(jnp.square(grouped - group_mean), axis=(0, 1, 2, 4), keepdims=True))
    normed = ((grouped - group_mean) * lax.rsqrt(group_var + 1e-06)).reshape(LF, 2 * LH, 2 * LW, CO)
    activated = jax.nn.silu(normed * norm_gain + norm_bias)
    return activated.transpose(1, 2, 3, 0).reshape(2 * LH, 2 * LW, CO * LF)
```

```python
import jax
import jax.numpy as jnp
from jax import lax
from jax.sharding import PartitionSpec as P

D = 3072
LC = 16
CO = 256
GROUPS = 32
ALL = ("section", "sp", "rep")
BLOCKS = ("section", "sp")


def valid_conv(volume, kernel, kernel_spec, precision_mode):
    front = jnp.concatenate([volume[:1], volume[:1], volume], axis=0)
    result = lax.conv_general_dilated(
        front[None],
        kernel,
        (1, 1, 1),
        "VALID",
        dimension_numbers=("NDHWC", kernel_spec, "NDHWC"),
        precision=precision_mode,
        preferred_element_type=jnp.float32,
    )
    return result[0]


def neighbours(stack, index, axis):
    pad = [(0, 0)] * stack.ndim
    pad[axis] = (1, 1)
    return lax.dynamic_slice_in_dim(jnp.pad(stack, pad), index, 3, axis)


def per_device(
    tokens,
    mod_scale,
    mod_shift,
    proj_weight,
    proj_bias,
    noisy_latent,
    in_weight,
    in_bias,
    conv_weight,
    conv_bias,
    norm_gain,
    norm_bias,
):
    n_sec, n_sp, n_rep = (lax.axis_size(a) for a in ALL)
    n_dev = n_sec * n_sp * n_rep
    sec, spi, rep = (lax.axis_index(a) for a in ALL)
    tok_frames, patch_rows, band_cols, local_width = tokens.shape
    frames, lat_rows, lat_cols, _ = noisy_latent.shape
    full_width = local_width * n_rep
    out_width = proj_weight.shape[0]

    scaled_weight = proj_weight * (1.0 + mod_scale)[None, :]
    shard_columns = jnp.sum(scaled_weight.reshape(out_width, n_rep, local_width), axis=2).T
    shift_column = (
        jnp.dot(
            proj_weight,
            mod_shift,
            precision=lax.Precision.HIGHEST,
            preferred_element_type=jnp.float32,
        )
        + proj_bias
    )
    local_weight = lax.dynamic_slice_in_dim(scaled_weight, rep * local_width, local_width, 1)

    shard_mean = jnp.mean(tokens, axis=-1, keepdims=True)
    centred = tokens - shard_mean
    shard_m2 = jnp.sum(centred * centred, axis=-1, keepdims=True)
    projected = lax.dot_general(
        centred,
        local_weight,
        (((3,), (1,)), ((), ())),
        precision=lax.Precision.HIGHEST,
        preferred_element_type=jnp.float32,
    )
    partial = jnp.concatenate([projected, shard_mean, shard_m2], axis=-1)

    slab = lat_rows // 2
    if patch_rows <= slab + 2:
        window = patch_rows
        per_slab = jnp.broadcast_to(partial[None], (n_sp,) + partial.shape)
    else:
        window = slab + 2
        padded = jnp.pad(partial, ((0, 0), (1, 1), (0, 0), (0, 0)))
        per_slab = jnp.stack([padded[:, p * slab : p * slab + window] for p in range(n_sp)])
    per_slab = per_slab.reshape(n_sp, -1)
    part_size = per_slab.shape[1]

    frame_rows = frames * lat_rows
    if frame_rows % n_rep == 0:
        share = frame_rows // n_rep
        latent_part = lax.dynamic_slice_in_dim(
            noisy_latent.reshape(frame_rows, -1), rep * share, share, 0
        ).reshape(-1)
    else:
        share = frame_rows
        latent_part = noisy_latent.reshape(-1)

    send = jnp.concatenate(
        [
            jnp.broadcast_to(per_slab[None, :, None], (n_sec, n_sp, n_rep, part_size)),
            jnp.broadcast_to(latent_part, (n_sec, n_sp, n_rep, latent_part.shape[0])),
        ],
        axis=-1,
    ).reshape(n_dev, -1)
    received = lax.all_to_all(send, ALL, 0, 0, tiled=False).reshape(n_sec, n_sp, n_rep, -1)

    parts = neighbours(received[..., :part_size], sec, 0).reshape(
        3, n_sp, n_rep, tok_frames, window, band_cols, out_width + 2
    )
    means = parts[..., out_width]
    mean = jnp.mean(means, axis=2)
    offsets = means - mean[:, :, None]
    m2 = jnp.sum(parts[..., out_width + 1], axis=2) + local_width * jnp.sum(
        offsets * offsets, axis=2
    )
    token_var = m2 / full_width
    centred_proj = jnp.sum(parts[..., :out_width], axis=2) + jnp.sum(
        offsets[..., None] * shard_columns.reshape(1, 1, n_rep, 1, 1, 1, out_width), axis=2
    )
    velocity = lax.rsqrt(token_var + 1e-06)[..., None] * centred_proj + shift_column
    patches = (
        velocity.reshape(3, frames, window, band_cols, LC, 2, 2)
        .transpose(1, 2, 5, 0, 3, 6, 4)
        .reshape(frames, 2 * window, 3 * 2 * band_cols, LC)
    )

    shares = neighbours(received[..., part_size:], sec, 0)
    if share == frame_rows:
        shares = shares[:, :, 0]
    latent = shares.reshape(3, n_sp, frames, lat_rows, lat_cols, LC)
    if window == patch_rows:
        latent = latent.transpose(2, 1, 3, 0, 4, 5).reshape(
            frames, n_sp * lat_rows, 3 * lat_cols, LC
        )
        clean = latent - 0.5 * patches
        clean = jnp.pad(clean, ((0, 0), (2, 2), (0, 0), (0, 0)))
        clean = lax.dynamic_slice_in_dim(clean, spi * lat_rows, lat_rows + 4, 1)
    else:
        latent = neighbours(latent.transpose(1, 2, 3, 0, 4, 5), spi, 0)
        latent = latent.transpose(1, 0, 2, 3, 4, 5).reshape(
            frames, 3 * lat_rows, 3 * lat_cols, LC
        )[:, lat_rows - 2 : 2 * lat_rows + 2]
        clean = latent - 0.5 * patches
    clean = clean[:, :, lat_cols - 2 : 2 * lat_cols + 2]

    row_global = spi * lat_rows - 2 + jnp.arange(lat_rows + 4)
    col_global = sec * lat_cols - 2 + jnp.arange(lat_cols + 4)
    row_inside = (row_global >= 0) & (row_global < lat_rows * n_sp)
    col_inside = (col_global >= 0) & (col_global < lat_cols * n_sec)
    clean = jnp.where(row_inside[None, :, None, None] & col_inside[None, None, :, None], clean, 0.0)

    inner_features = valid_conv(clean, in_weight, "DHWIO", lax.Precision.HIGHEST) + in_bias
    inside = row_inside[None, 1:-1, None, None] & col_inside[None, None, 1:-1, None]
    features = jnp.where(inside, inner_features, 0.0).astype(jnp.bfloat16)
    upsampled = jnp.repeat(jnp.repeat(features, 2, axis=1), 2, axis=2)[:, 1:-1, 1:-1, :]
    mixed = valid_conv(upsampled, conv_weight, "DHWOI", None) + conv_bias

    group_size = CO // GROUPS
    local_groups = mixed.shape[-1] // group_size
    grouped = mixed.reshape(-1, local_groups, group_size)
    block_count = grouped.shape[0] * group_size
    block_mean = jnp.sum(grouped, axis=(0, 2)) / block_count
    deviation = grouped - block_mean[None, :, None]
    block_m2 = jnp.sum(deviation * deviation, axis=(0, 2))
    n_blocks = n_sec * n_sp
    stats = jnp.broadcast_to(
        jnp.concatenate([block_mean, block_m2])[None], (n_blocks, 2 * local_groups)
    )
    stats = lax.all_to_all(stats, BLOCKS, 0, 0, tiled=False)
    group_mean = jnp.mean(stats[:, :local_groups], axis=0)
    mean_offsets = stats[:, :local_groups] - group_mean[None]
    group_var = (
        jnp.sum(stats[:, local_groups:], axis=0)
        + block_count * jnp.sum(mean_offsets * mean_offsets, axis=0)
    ) / (block_count * n_blocks)

    normed = (
        (grouped - group_mean[None, :, None]) * lax.rsqrt(group_var + 1e-06)[None, :, None]
    ).reshape(mixed.shape)
    activated = jax.nn.silu(normed * norm_gain + norm_bias)
    out_rows, out_cols, out_chan = (activated.shape[1], activated.shape[2], activated.shape[3])
    return activated.transpose(1, 2, 3, 0).reshape(out_rows, out_cols, out_chan * frames)


def solution(mesh):
    return jax.shard_map(
        per_device,
        mesh=mesh,
        in_specs=(
            P("sp", None, "section", "rep"),
            P(),
            P(),
            P(),
            P(),
            P(None, "sp", "section", None),
            P(),
            P(),
            P(None, None, None, "rep", None),
            P("rep"),
            P("rep"),
            P("rep"),
        ),
        out_specs=P("sp", "section", "rep"),
        check_vma=False,
    )
```

```python
import jax
import jax.numpy as jnp
from jax import lax
from jax.sharding import PartitionSpec as P

D = 3072
LC = 16
CO = 256
GROUPS = 32
ALL = ("section", "sp", "rep")
BLOCKS = ("section", "sp")


def valid_conv(volume, kernel, kernel_spec, precision_mode):
    front = jnp.concatenate([volume[:1], volume[:1], volume], axis=0)
    result = lax.conv_general_dilated(
        front[None],
        kernel,
        (1, 1, 1),
        "VALID",
        dimension_numbers=("NDHWC", kernel_spec, "NDHWC"),
        precision=precision_mode,
        preferred_element_type=jnp.float32,
    )
    return result[0]


def neighbours(stack, index, axis):
    pad = [(0, 0)] * stack.ndim
    pad[axis] = (1, 1)
    return lax.dynamic_slice_in_dim(jnp.pad(stack, pad), index, 3, axis)


def per_device(
    tokens,
    mod_scale,
    mod_shift,
    proj_weight,
    proj_bias,
    noisy_latent,
    in_weight,
    in_bias,
    conv_weight,
    conv_bias,
    norm_gain,
    norm_bias,
):
    n_sec, n_sp, n_rep = (lax.axis_size(a) for a in ALL)
    n_dev = n_sec * n_sp * n_rep
    sec, spi, rep = (lax.axis_index(a) for a in ALL)
    tok_frames, patch_rows, band_cols, local_width = tokens.shape
    frames, lat_rows, lat_cols, _ = noisy_latent.shape
    full_width = local_width * n_rep
    out_width = proj_weight.shape[0]

    low = rep * local_width
    local_weight = lax.dynamic_slice_in_dim(proj_weight, low, local_width, 1) * (
        1.0 + lax.dynamic_slice_in_dim(mod_scale, low, local_width, 0)
    )[None, :]

    rows = tokens.reshape(-1, local_width)
    shard_mean = jnp.mean(rows, axis=-1, keepdims=True)
    centred = rows - shard_mean
    shard_m2 = jnp.sum(centred * centred, axis=-1, keepdims=True)
    projected = lax.dot_general(
        centred,
        local_weight,
        (((1,), (1,)), ((), ())),
        precision=lax.Precision.HIGHEST,
        preferred_element_type=jnp.float32,
    )
    partial = jnp.concatenate([projected, shard_mean, shard_m2], axis=-1).reshape(
        tok_frames, patch_rows, band_cols, out_width + 2
    )

    slab = lat_rows // 2
    if patch_rows <= slab + 2:
        window = patch_rows
        per_slab = jnp.broadcast_to(partial[None], (n_sp,) + partial.shape)
    else:
        window = slab + 2
        padded = jnp.pad(partial, ((0, 0), (1, 1), (0, 0), (0, 0)))
        per_slab = jnp.stack([padded[:, p * slab : p * slab + window] for p in range(n_sp)])
    per_slab = per_slab.reshape(n_sp, -1)
    part_size = per_slab.shape[1]

    frame_rows = frames * lat_rows
    if frame_rows % n_rep == 0:
        share = frame_rows // n_rep
        latent_part = lax.dynamic_slice_in_dim(
            noisy_latent.reshape(frame_rows, -1), rep * share, share, 0
        ).reshape(-1)
    else:
        share = frame_rows
        latent_part = noisy_latent.reshape(-1)

    send = jnp.concatenate(
        [
            jnp.broadcast_to(per_slab[None, :, None], (n_sec, n_sp, n_rep, part_size)),
            jnp.broadcast_to(latent_part, (n_sec, n_sp, n_rep, latent_part.shape[0])),
        ],
        axis=-1,
    ).reshape(n_dev, -1)
    received = lax.all_to_all(send, ALL, 0, 0, tiled=False).reshape(n_sec, n_sp, n_rep, -1)

    scaled_weight = proj_weight * (1.0 + mod_scale)[None, :]
    shard_columns = jnp.sum(scaled_weight.reshape(out_width, n_rep, local_width), axis=2).T
    shift_column = (
        jnp.dot(
            proj_weight,
            mod_shift,
            precision=lax.Precision.HIGHEST,
            preferred_element_type=jnp.float32,
        )
        + proj_bias
    )
    parts = neighbours(received[..., :part_size], sec, 0).reshape(
        3, n_sp, n_rep, tok_frames, window, band_cols, out_width + 2
    )
    means = parts[..., out_width]
    mean = jnp.mean(means, axis=2)
    offsets = means - mean[:, :, None]
    m2 = jnp.sum(parts[..., out_width + 1], axis=2) + local_width * jnp.sum(
        offsets * offsets, axis=2
    )
    token_var = m2 / full_width
    centred_proj = jnp.sum(parts[..., :out_width], axis=2) + jnp.sum(
        offsets[..., None] * shard_columns.reshape(1, 1, n_rep, 1, 1, 1, out_width), axis=2
    )
    velocity = lax.rsqrt(token_var + 1e-06)[..., None] * centred_proj + shift_column
    patches = (
        velocity.reshape(3, frames, window, band_cols, LC, 2, 2)
        .transpose(1, 2, 5, 0, 3, 6, 4)
        .reshape(frames, 2 * window, 3 * 2 * band_cols, LC)
    )

    shares = neighbours(received[..., part_size:], sec, 0)
    if share == frame_rows:
        shares = shares[:, :, 0]
    latent = shares.reshape(3, n_sp, frames, lat_rows, lat_cols, LC)
    if window == patch_rows:
        latent = latent.transpose(2, 1, 3, 0, 4, 5).reshape(
            frames, n_sp * lat_rows, 3 * lat_cols, LC
        )
        clean = latent - 0.5 * patches
        clean = jnp.pad(clean, ((0, 0), (2, 2), (0, 0), (0, 0)))
        clean = lax.dynamic_slice_in_dim(clean, spi * lat_rows, lat_rows + 4, 1)
    else:
        latent = neighbours(latent.transpose(1, 2, 3, 0, 4, 5), spi, 0)
        latent = latent.transpose(1, 0, 2, 3, 4, 5).reshape(
            frames, 3 * lat_rows, 3 * lat_cols, LC
        )[:, lat_rows - 2 : 2 * lat_rows + 2]
        clean = latent - 0.5 * patches
    clean = clean[:, :, lat_cols - 2 : 2 * lat_cols + 2]

    row_global = spi * lat_rows - 2 + jnp.arange(lat_rows + 4)
    col_global = sec * lat_cols - 2 + jnp.arange(lat_cols + 4)
    row_inside = (row_global >= 0) & (row_global < lat_rows * n_sp)
    col_inside = (col_global >= 0) & (col_global < lat_cols * n_sec)
    clean = jnp.where(row_inside[None, :, None, None] & col_inside[None, None, :, None], clean, 0.0)

    inner_features = valid_conv(clean, in_weight, "DHWIO", lax.Precision.HIGH) + in_bias
    inside = row_inside[None, 1:-1, None, None] & col_inside[None, None, 1:-1, None]
    features = jnp.where(inside, inner_features, 0.0).astype(jnp.bfloat16)
    upsampled = jnp.repeat(jnp.repeat(features, 2, axis=1), 2, axis=2)[:, 1:-1, 1:-1, :]
    mixed = valid_conv(upsampled, conv_weight, "DHWOI", None) + conv_bias

    group_size = CO // GROUPS
    local_groups = mixed.shape[-1] // group_size
    grouped = mixed.reshape(-1, local_groups, group_size)
    block_count = grouped.shape[0] * group_size
    block_mean = jnp.sum(grouped, axis=(0, 2)) / block_count
    deviation = grouped - block_mean[None, :, None]
    block_m2 = jnp.sum(deviation * deviation, axis=(0, 2))
    n_blocks = n_sec * n_sp
    stats = jnp.broadcast_to(
        jnp.concatenate([block_mean, block_m2])[None], (n_blocks, 2 * local_groups)
    )
    stats = lax.all_to_all(stats, BLOCKS, 0, 0, tiled=False)
    group_mean = jnp.mean(stats[:, :local_groups], axis=0)
    mean_offsets = stats[:, :local_groups] - group_mean[None]
    group_var = (
        jnp.sum(stats[:, local_groups:], axis=0)
        + block_count * jnp.sum(mean_offsets * mean_offsets, axis=0)
    ) / (block_count * n_blocks)

    normed = (
        (grouped - group_mean[None, :, None]) * lax.rsqrt(group_var + 1e-06)[None, :, None]
    ).reshape(mixed.shape)
    activated = jax.nn.silu(normed * norm_gain + norm_bias)
    out_rows, out_cols, out_chan = (activated.shape[1], activated.shape[2], activated.shape[3])
    return activated.transpose(1, 2, 3, 0).reshape(out_rows, out_cols, out_chan * frames)


def solution(mesh):
    return jax.shard_map(
        per_device,
        mesh=mesh,
        in_specs=(
            P("sp", None, "section", "rep"),
            P(),
            P(),
            P(),
            P(),
            P(None, "sp", "section", None),
            P(),
            P(),
            P(None, None, None, "rep", None),
            P("rep"),
            P("rep"),
            P("rep"),
        ),
        out_specs=P("sp", "section", "rep"),
        check_vma=False,
    )
```

```python
import jax
import jax.numpy as jnp
from jax import lax
from jax.experimental import pallas as pl
from jax.experimental.pallas import tpu as pltpu
from jax.sharding import PartitionSpec as P

D = 3072
LC = 16
CO = 256
GROUPS = 32
ALL = ("section", "sp", "rep")
BLOCKS = ("section", "sp")


def valid_conv(volume, kernel, kernel_spec, precision_mode):
    front = jnp.concatenate([volume[:1], volume[:1], volume], axis=0)
    result = lax.conv_general_dilated(
        front[None],
        kernel,
        (1, 1, 1),
        "VALID",
        dimension_numbers=("NDHWC", kernel_spec, "NDHWC"),
        precision=precision_mode,
        preferred_element_type=jnp.float32,
    )
    return result[0]


def shard_kernel(rep_ref, tok_ref, weight_ref, scale_ref, proj_ref, mean_ref, m2_ref):
    weight = weight_ref[...] * (1.0 + scale_ref[...])
    for frame in range(tok_ref.shape[0]):
        for row in range(tok_ref.shape[1]):
            x = tok_ref[frame, row]
            mean = jnp.mean(x, axis=1, keepdims=True)
            centred = x - mean
            proj_ref[frame, row] = lax.dot_general(
                centred,
                weight,
                (((1,), (1,)), ((), ())),
                precision=lax.Precision.HIGHEST,
                preferred_element_type=jnp.float32,
            )
            mean_ref[frame, row] = mean
            m2_ref[frame, row] = jnp.sum(centred * centred, axis=1, keepdims=True)


def shard_moments(tokens, proj_weight, mod_scale, rep):
    tok_frames, patch_rows, band_cols, local_width = tokens.shape
    out_width = proj_weight.shape[0]
    whole = lambda i, r: (0, 0, 0, 0)
    lead = (tok_frames, patch_rows, band_cols)
    return pl.pallas_call(
        shard_kernel,
        grid_spec=pltpu.PrefetchScalarGridSpec(
            num_scalar_prefetch=1,
            grid=(1,),
            in_specs=[
                pl.BlockSpec(tokens.shape, whole),
                pl.BlockSpec((out_width, local_width), lambda i, r: (0, r[0])),
                pl.BlockSpec((1, local_width), lambda i, r: (0, r[0])),
            ],
            out_specs=[
                pl.BlockSpec(lead + (out_width,), whole),
                pl.BlockSpec(lead + (1,), whole),
                pl.BlockSpec(lead + (1,), whole),
            ],
        ),
        out_shape=[
            jax.ShapeDtypeStruct(lead + (out_width,), jnp.float32),
            jax.ShapeDtypeStruct(lead + (1,), jnp.float32),
            jax.ShapeDtypeStruct(lead + (1,), jnp.float32),
        ],
    )(rep.reshape(1).astype(jnp.int32), tokens, proj_weight, mod_scale.reshape(1, -1))


def neighbours(stack, index, axis):
    pad = [(0, 0)] * stack.ndim
    pad[axis] = (1, 1)
    return lax.dynamic_slice_in_dim(jnp.pad(stack, pad), index, 3, axis)


def per_device(
    tokens,
    mod_scale,
    mod_shift,
    proj_weight,
    proj_bias,
    noisy_latent,
    in_weight,
    in_bias,
    conv_weight,
    conv_bias,
    norm_gain,
    norm_bias,
):
    n_sec, n_sp, n_rep = (lax.axis_size(a) for a in ALL)
    n_dev = n_sec * n_sp * n_rep
    sec, spi, rep = (lax.axis_index(a) for a in ALL)
    tok_frames, patch_rows, band_cols, local_width = tokens.shape
    frames, lat_rows, lat_cols, _ = noisy_latent.shape
    full_width = local_width * n_rep
    out_width = proj_weight.shape[0]

    projected, shard_mean, shard_m2 = shard_moments(tokens, proj_weight, mod_scale, rep)
    partial = jnp.concatenate([projected, shard_mean, shard_m2], axis=-1)

    slab = lat_rows // 2
    if patch_rows <= slab + 2:
        window = patch_rows
        per_slab = jnp.broadcast_to(partial[None], (n_sp,) + partial.shape)
    else:
        window = slab + 2
        padded = jnp.pad(partial, ((0, 0), (1, 1), (0, 0), (0, 0)))
        per_slab = jnp.stack([padded[:, p * slab : p * slab + window] for p in range(n_sp)])
    per_slab = per_slab.reshape(n_sp, -1)
    part_size = per_slab.shape[1]

    frame_rows = frames * lat_rows
    if frame_rows % n_rep == 0:
        share = frame_rows // n_rep
        latent_part = lax.dynamic_slice_in_dim(
            noisy_latent.reshape(frame_rows, -1), rep * share, share, 0
        ).reshape(-1)
    else:
        share = frame_rows
        latent_part = noisy_latent.reshape(-1)

    send = jnp.concatenate(
        [
            jnp.broadcast_to(per_slab[None, :, None], (n_sec, n_sp, n_rep, part_size)),
            jnp.broadcast_to(latent_part, (n_sec, n_sp, n_rep, latent_part.shape[0])),
        ],
        axis=-1,
    ).reshape(n_dev, -1)
    received = lax.all_to_all(send, ALL, 0, 0, tiled=False).reshape(n_sec, n_sp, n_rep, -1)

    scaled_weight = proj_weight * (1.0 + mod_scale)[None, :]
    shard_columns = jnp.sum(scaled_weight.reshape(out_width, n_rep, local_width), axis=2).T
    shift_column = (
        jnp.dot(
            proj_weight,
            mod_shift,
            precision=lax.Precision.HIGHEST,
            preferred_element_type=jnp.float32,
        )
        + proj_bias
    )
    parts = neighbours(received[..., :part_size], sec, 0).reshape(
        3, n_sp, n_rep, tok_frames, window, band_cols, out_width + 2
    )
    means = parts[..., out_width]
    mean = jnp.mean(means, axis=2)
    offsets = means - mean[:, :, None]
    m2 = jnp.sum(parts[..., out_width + 1], axis=2) + local_width * jnp.sum(
        offsets * offsets, axis=2
    )
    token_var = m2 / full_width
    centred_proj = jnp.sum(parts[..., :out_width], axis=2) + jnp.sum(
        offsets[..., None] * shard_columns.reshape(1, 1, n_rep, 1, 1, 1, out_width), axis=2
    )
    velocity = lax.rsqrt(token_var + 1e-06)[..., None] * centred_proj + shift_column
    patches = (
        velocity.reshape(3, frames, window, band_cols, LC, 2, 2)
        .transpose(1, 2, 5, 0, 3, 6, 4)
        .reshape(frames, 2 * window, 3 * 2 * band_cols, LC)
    )

    shares = neighbours(received[..., part_size:], sec, 0)
    if share == frame_rows:
        shares = shares[:, :, 0]
    latent = shares.reshape(3, n_sp, frames, lat_rows, lat_cols, LC)
    if window == patch_rows:
        latent = latent.transpose(2, 1, 3, 0, 4, 5).reshape(
            frames, n_sp * lat_rows, 3 * lat_cols, LC
        )
        clean = latent - 0.5 * patches
        clean = jnp.pad(clean, ((0, 0), (2, 2), (0, 0), (0, 0)))
        clean = lax.dynamic_slice_in_dim(clean, spi * lat_rows, lat_rows + 4, 1)
    else:
        latent = neighbours(latent.transpose(1, 2, 3, 0, 4, 5), spi, 0)
        latent = latent.transpose(1, 0, 2, 3, 4, 5).reshape(
            frames, 3 * lat_rows, 3 * lat_cols, LC
        )[:, lat_rows - 2 : 2 * lat_rows + 2]
        clean = latent - 0.5 * patches
    clean = clean[:, :, lat_cols - 2 : 2 * lat_cols + 2]

    row_global = spi * lat_rows - 2 + jnp.arange(lat_rows + 4)
    col_global = sec * lat_cols - 2 + jnp.arange(lat_cols + 4)
    row_inside = (row_global >= 0) & (row_global < lat_rows * n_sp)
    col_inside = (col_global >= 0) & (col_global < lat_cols * n_sec)
    clean = jnp.where(row_inside[None, :, None, None] & col_inside[None, None, :, None], clean, 0.0)

    inner_features = valid_conv(clean, in_weight, "DHWIO", lax.Precision.HIGH) + in_bias
    inside = row_inside[None, 1:-1, None, None] & col_inside[None, None, 1:-1, None]
    features = jnp.where(inside, inner_features, 0.0).astype(jnp.bfloat16)
    upsampled = jnp.repeat(jnp.repeat(features, 2, axis=1), 2, axis=2)[:, 1:-1, 1:-1, :]
    mixed = valid_conv(upsampled, conv_weight, "DHWOI", None) + conv_bias

    group_size = CO // GROUPS
    local_groups = mixed.shape[-1] // group_size
    grouped = mixed.reshape(-1, local_groups, group_size)
    block_count = grouped.shape[0] * group_size
    block_mean = jnp.sum(grouped, axis=(0, 2)) / block_count
    deviation = grouped - block_mean[None, :, None]
    block_m2 = jnp.sum(deviation * deviation, axis=(0, 2))
    n_blocks = n_sec * n_sp
    stats = jnp.broadcast_to(
        jnp.concatenate([block_mean, block_m2])[None], (n_blocks, 2 * local_groups)
    )
    stats = lax.all_to_all(stats, BLOCKS, 0, 0, tiled=False)
    group_mean = jnp.mean(stats[:, :local_groups], axis=0)
    mean_offsets = stats[:, :local_groups] - group_mean[None]
    group_var = (
        jnp.sum(stats[:, local_groups:], axis=0)
        + block_count * jnp.sum(mean_offsets * mean_offsets, axis=0)
    ) / (block_count * n_blocks)

    normed = (
        (grouped - group_mean[None, :, None]) * lax.rsqrt(group_var + 1e-06)[None, :, None]
    ).reshape(mixed.shape)
    activated = jax.nn.silu(normed * norm_gain + norm_bias)
    out_rows, out_cols, out_chan = (activated.shape[1], activated.shape[2], activated.shape[3])
    return activated.transpose(1, 2, 3, 0).reshape(out_rows, out_cols, out_chan * frames)


def solution(mesh):
    return jax.shard_map(
        per_device,
        mesh=mesh,
        in_specs=(
            P("sp", None, "section", "rep"),
            P(),
            P(),
            P(),
            P(),
            P(None, "sp", "section", None),
            P(),
            P(),
            P(None, None, None, "rep", None),
            P("rep"),
            P("rep"),
            P("rep"),
        ),
        out_specs=P("sp", "section", "rep"),
        check_vma=False,
    )
```

```python
import jax
import jax.numpy as jnp
from jax import lax
from jax.experimental import pallas as pl
from jax.experimental.pallas import tpu as pltpu
from jax.sharding import PartitionSpec as P

D = 3072
LC = 16
CO = 256
GROUPS = 32
ALL = ("section", "sp", "rep")
BLOCKS = ("section", "sp")


def valid_conv(volume, kernel, kernel_spec, precision_mode):
    front = jnp.concatenate([volume[:1], volume[:1], volume], axis=0)
    result = lax.conv_general_dilated(
        front[None],
        kernel,
        (1, 1, 1),
        "VALID",
        dimension_numbers=("NDHWC", kernel_spec, "NDHWC"),
        precision=precision_mode,
        preferred_element_type=jnp.float32,
    )
    return result[0]


def shard_kernel(rep_ref, tok_ref, weight_ref, scale_ref, proj_ref, mean_ref, m2_ref):
    weight = weight_ref[...] * (1.0 + scale_ref[...])
    for frame in range(tok_ref.shape[0]):
        for row in range(tok_ref.shape[2]):
            x = tok_ref[frame, :, row, :]
            mean = jnp.mean(x, axis=1, keepdims=True)
            centred = x - mean
            proj_ref[frame, row] = lax.dot_general(
                centred,
                weight,
                (((1,), (1,)), ((), ())),
                precision=lax.Precision.HIGHEST,
                preferred_element_type=jnp.float32,
            )
            mean_ref[frame, row] = mean
            m2_ref[frame, row] = jnp.sum(centred * centred, axis=1, keepdims=True)


def shard_moments(tokens, proj_weight, mod_scale, rep):
    tok_frames, patch_rows, band_cols, local_width = tokens.shape
    out_width = proj_weight.shape[0]
    whole = lambda i, r: (0, 0, 0, 0)
    lead = (tok_frames, patch_rows, band_cols)
    return pl.pallas_call(
        shard_kernel,
        grid_spec=pltpu.PrefetchScalarGridSpec(
            num_scalar_prefetch=1,
            grid=(1,),
            in_specs=[
                pl.BlockSpec((tok_frames, band_cols, patch_rows, local_width), whole),
                pl.BlockSpec((out_width, local_width), lambda i, r: (0, r[0])),
                pl.BlockSpec((1, local_width), lambda i, r: (0, r[0])),
            ],
            out_specs=[
                pl.BlockSpec(lead + (out_width,), whole),
                pl.BlockSpec(lead + (1,), whole),
                pl.BlockSpec(lead + (1,), whole),
            ],
        ),
        out_shape=[
            jax.ShapeDtypeStruct(lead + (out_width,), jnp.float32),
            jax.ShapeDtypeStruct(lead + (1,), jnp.float32),
            jax.ShapeDtypeStruct(lead + (1,), jnp.float32),
        ],
    )(
        rep.reshape(1).astype(jnp.int32),
        tokens.transpose(0, 2, 1, 3),
        proj_weight,
        mod_scale.reshape(1, -1),
    )


def neighbours(stack, index, axis):
    pad = [(0, 0)] * stack.ndim
    pad[axis] = (1, 1)
    return lax.dynamic_slice_in_dim(jnp.pad(stack, pad), index, 3, axis)


def per_device(
    tokens,
    mod_scale,
    mod_shift,
    proj_weight,
    proj_bias,
    noisy_latent,
    in_weight,
    in_bias,
    conv_weight,
    conv_bias,
    norm_gain,
    norm_bias,
):
    n_sec, n_sp, n_rep = (lax.axis_size(a) for a in ALL)
    n_dev = n_sec * n_sp * n_rep
    sec, spi, rep = (lax.axis_index(a) for a in ALL)
    tok_frames, patch_rows, band_cols, local_width = tokens.shape
    frames, lat_rows, lat_cols, _ = noisy_latent.shape
    full_width = local_width * n_rep
    out_width = proj_weight.shape[0]

    projected, shard_mean, shard_m2 = shard_moments(tokens, proj_weight, mod_scale, rep)
    partial = jnp.concatenate([projected, shard_mean, shard_m2], axis=-1)

    slab = lat_rows // 2
    if patch_rows <= slab + 2:
        window = patch_rows
        per_slab = jnp.broadcast_to(partial[None], (n_sp,) + partial.shape)
    else:
        window = slab + 2
        padded = jnp.pad(partial, ((0, 0), (1, 1), (0, 0), (0, 0)))
        per_slab = jnp.stack([padded[:, p * slab : p * slab + window] for p in range(n_sp)])
    per_slab = per_slab.reshape(n_sp, -1)
    part_size = per_slab.shape[1]

    frame_rows = frames * lat_rows
    if frame_rows % n_rep == 0:
        share = frame_rows // n_rep
        latent_part = lax.dynamic_slice_in_dim(
            noisy_latent.reshape(frame_rows, -1), rep * share, share, 0
        ).reshape(-1)
    else:
        share = frame_rows
        latent_part = noisy_latent.reshape(-1)

    send = jnp.concatenate(
        [
            jnp.broadcast_to(per_slab[None, :, None], (n_sec, n_sp, n_rep, part_size)),
            jnp.broadcast_to(latent_part, (n_sec, n_sp, n_rep, latent_part.shape[0])),
        ],
        axis=-1,
    ).reshape(n_dev, -1)
    received = lax.all_to_all(send, ALL, 0, 0, tiled=False).reshape(n_sec, n_sp, n_rep, -1)

    scaled_weight = proj_weight * (1.0 + mod_scale)[None, :]
    shard_columns = jnp.sum(scaled_weight.reshape(out_width, n_rep, local_width), axis=2).T
    shift_column = (
        jnp.dot(
            proj_weight,
            mod_shift,
            precision=lax.Precision.HIGHEST,
            preferred_element_type=jnp.float32,
        )
        + proj_bias
    )
    parts = neighbours(received[..., :part_size], sec, 0).reshape(
        3, n_sp, n_rep, tok_frames, window, band_cols, out_width + 2
    )
    means = parts[..., out_width]
    mean = jnp.mean(means, axis=2)
    offsets = means - mean[:, :, None]
    m2 = jnp.sum(parts[..., out_width + 1], axis=2) + local_width * jnp.sum(
        offsets * offsets, axis=2
    )
    token_var = m2 / full_width
    centred_proj = jnp.sum(parts[..., :out_width], axis=2) + jnp.sum(
        offsets[..., None] * shard_columns.reshape(1, 1, n_rep, 1, 1, 1, out_width), axis=2
    )
    velocity = lax.rsqrt(token_var + 1e-06)[..., None] * centred_proj + shift_column
    patches = (
        velocity.reshape(3, frames, window, band_cols, LC, 2, 2)
        .transpose(1, 2, 5, 0, 3, 6, 4)
        .reshape(frames, 2 * window, 3 * 2 * band_cols, LC)
    )

    shares = neighbours(received[..., part_size:], sec, 0)
    if share == frame_rows:
        shares = shares[:, :, 0]
    latent = shares.reshape(3, n_sp, frames, lat_rows, lat_cols, LC)
    if window == patch_rows:
        latent = latent.transpose(2, 1, 3, 0, 4, 5).reshape(
            frames, n_sp * lat_rows, 3 * lat_cols, LC
        )
        clean = latent - 0.5 * patches
        clean = jnp.pad(clean, ((0, 0), (2, 2), (0, 0), (0, 0)))
        clean = lax.dynamic_slice_in_dim(clean, spi * lat_rows, lat_rows + 4, 1)
    else:
        latent = neighbours(latent.transpose(1, 2, 3, 0, 4, 5), spi, 0)
        latent = latent.transpose(1, 0, 2, 3, 4, 5).reshape(
            frames, 3 * lat_rows, 3 * lat_cols, LC
        )[:, lat_rows - 2 : 2 * lat_rows + 2]
        clean = latent - 0.5 * patches
    clean = clean[:, :, lat_cols - 2 : 2 * lat_cols + 2]

    row_global = spi * lat_rows - 2 + jnp.arange(lat_rows + 4)
    col_global = sec * lat_cols - 2 + jnp.arange(lat_cols + 4)
    row_inside = (row_global >= 0) & (row_global < lat_rows * n_sp)
    col_inside = (col_global >= 0) & (col_global < lat_cols * n_sec)
    clean = jnp.where(row_inside[None, :, None, None] & col_inside[None, None, :, None], clean, 0.0)

    inner_features = valid_conv(clean, in_weight, "DHWIO", lax.Precision.HIGH) + in_bias
    inside = row_inside[None, 1:-1, None, None] & col_inside[None, None, 1:-1, None]
    features = jnp.where(inside, inner_features, 0.0).astype(jnp.bfloat16)
    upsampled = jnp.repeat(jnp.repeat(features, 2, axis=1), 2, axis=2)[:, 1:-1, 1:-1, :]
    mixed = valid_conv(upsampled, conv_weight, "DHWOI", None) + conv_bias

    group_size = CO // GROUPS
    local_groups = mixed.shape[-1] // group_size
    grouped = mixed.reshape(-1, local_groups, group_size)
    block_count = grouped.shape[0] * group_size
    block_mean = jnp.sum(grouped, axis=(0, 2)) / block_count
    deviation = grouped - block_mean[None, :, None]
    block_m2 = jnp.sum(deviation * deviation, axis=(0, 2))
    n_blocks = n_sec * n_sp
    stats = jnp.broadcast_to(
        jnp.concatenate([block_mean, block_m2])[None], (n_blocks, 2 * local_groups)
    )
    stats = lax.all_to_all(stats, BLOCKS, 0, 0, tiled=False)
    group_mean = jnp.mean(stats[:, :local_groups], axis=0)
    mean_offsets = stats[:, :local_groups] - group_mean[None]
    group_var = (
        jnp.sum(stats[:, local_groups:], axis=0)
        + block_count * jnp.sum(mean_offsets * mean_offsets, axis=0)
    ) / (block_count * n_blocks)

    normed = (
        (grouped - group_mean[None, :, None]) * lax.rsqrt(group_var + 1e-06)[None, :, None]
    ).reshape(mixed.shape)
    activated = jax.nn.silu(normed * norm_gain + norm_bias)
    out_rows, out_cols, out_chan = (activated.shape[1], activated.shape[2], activated.shape[3])
    return activated.transpose(1, 2, 3, 0).reshape(out_rows, out_cols, out_chan * frames)


def solution(mesh):
    return jax.shard_map(
        per_device,
        mesh=mesh,
        in_specs=(
            P("sp", None, "section", "rep"),
            P(),
            P(),
            P(),
            P(),
            P(None, "sp", "section", None),
            P(),
            P(),
            P(None, None, None, "rep", None),
            P("rep"),
            P("rep"),
            P("rep"),
        ),
        out_specs=P("sp", "section", "rep"),
        check_vma=False,
    )
```

```python
import jax
import jax.numpy as jnp
from jax import lax
from jax.experimental import pallas as pl
from jax.experimental.pallas import tpu as pltpu
from jax.sharding import PartitionSpec as P

D = 3072
LC = 16
CO = 256
GROUPS = 32
ALL = ("section", "sp", "rep")
BLOCKS = ("section", "sp")


def valid_conv(volume, kernel, kernel_spec, precision_mode):
    front = jnp.concatenate([volume[:1], volume[:1], volume], axis=0)
    result = lax.conv_general_dilated(
        front[None],
        kernel,
        (1, 1, 1),
        "VALID",
        dimension_numbers=("NDHWC", kernel_spec, "NDHWC"),
        precision=precision_mode,
        preferred_element_type=jnp.float32,
    )
    return result[0]


def shard_kernel(rep_ref, tok_ref, weight_ref, scale_ref, out_ref):
    weight = weight_ref[...] * (1.0 + scale_ref[...])
    for frame in range(tok_ref.shape[0]):
        for row in range(tok_ref.shape[2]):
            x = tok_ref[frame, :, row, :]
            mean = jnp.mean(x, axis=1, keepdims=True)
            centred = x - mean
            width = weight.shape[0]
            out_ref[frame, row, :, :width] = lax.dot_general(
                centred,
                weight,
                (((1,), (1,)), ((), ())),
                precision=lax.Precision.HIGHEST,
                preferred_element_type=jnp.float32,
            )
            out_ref[frame, row, :, width : width + 1] = mean
            out_ref[frame, row, :, width + 1 : width + 2] = jnp.sum(
                centred * centred, axis=1, keepdims=True
            )


def shard_moments(tokens, proj_weight, mod_scale, rep):
    tok_frames, patch_rows, band_cols, local_width = tokens.shape
    out_width = proj_weight.shape[0]
    whole = lambda i, r: (0, 0, 0, 0)
    lead = (tok_frames, patch_rows, band_cols)
    return pl.pallas_call(
        shard_kernel,
        grid_spec=pltpu.PrefetchScalarGridSpec(
            num_scalar_prefetch=1,
            grid=(1,),
            in_specs=[
                pl.BlockSpec((tok_frames, band_cols, patch_rows, local_width), whole),
                pl.BlockSpec((out_width, local_width), lambda i, r: (0, r[0])),
                pl.BlockSpec((1, local_width), lambda i, r: (0, r[0])),
            ],
            out_specs=pl.BlockSpec(lead + (out_width + 2,), whole),
        ),
        out_shape=jax.ShapeDtypeStruct(lead + (out_width + 2,), jnp.float32),
    )(
        rep.reshape(1).astype(jnp.int32),
        tokens.transpose(0, 2, 1, 3),
        proj_weight,
        mod_scale.reshape(1, -1),
    )


def neighbours(stack, index, axis):
    pad = [(0, 0)] * stack.ndim
    pad[axis] = (1, 1)
    return lax.dynamic_slice_in_dim(jnp.pad(stack, pad), index, 3, axis)


def per_device(
    tokens,
    mod_scale,
    mod_shift,
    proj_weight,
    proj_bias,
    noisy_latent,
    in_weight,
    in_bias,
    conv_weight,
    conv_bias,
    norm_gain,
    norm_bias,
):
    n_sec, n_sp, n_rep = (lax.axis_size(a) for a in ALL)
    n_dev = n_sec * n_sp * n_rep
    sec, spi, rep = (lax.axis_index(a) for a in ALL)
    tok_frames, patch_rows, band_cols, local_width = tokens.shape
    frames, lat_rows, lat_cols, _ = noisy_latent.shape
    full_width = local_width * n_rep
    out_width = proj_weight.shape[0]

    partial = shard_moments(tokens, proj_weight, mod_scale, rep)

    slab = lat_rows // 2
    if patch_rows <= slab + 2:
        window = patch_rows
        per_slab = jnp.broadcast_to(partial[None], (n_sp,) + partial.shape)
    else:
        window = slab + 2
        padded = jnp.pad(partial, ((0, 0), (1, 1), (0, 0), (0, 0)))
        per_slab = jnp.stack([padded[:, p * slab : p * slab + window] for p in range(n_sp)])
    per_slab = per_slab.reshape(n_sp, -1)
    part_size = per_slab.shape[1]

    lines = frames * lat_cols
    stored = noisy_latent.transpose(0, 2, 1, 3).reshape(lines, lat_rows, LC)
    if lines % n_rep == 0:
        share = lines // n_rep
        latent_part = lax.dynamic_slice_in_dim(stored, rep * share, share, 0).reshape(-1)
    else:
        share = lines
        latent_part = stored.reshape(-1)

    send = jnp.concatenate(
        [
            jnp.broadcast_to(per_slab[None, :, None], (n_sec, n_sp, n_rep, part_size)),
            jnp.broadcast_to(latent_part, (n_sec, n_sp, n_rep, latent_part.shape[0])),
        ],
        axis=-1,
    ).reshape(n_dev, -1)
    received = lax.all_to_all(send, ALL, 0, 0, tiled=False).reshape(n_sec, n_sp, n_rep, -1)

    scaled_weight = proj_weight * (1.0 + mod_scale)[None, :]
    shard_columns = jnp.sum(scaled_weight.reshape(out_width, n_rep, local_width), axis=2).T
    shift_column = (
        jnp.dot(
            proj_weight,
            mod_shift,
            precision=lax.Precision.HIGHEST,
            preferred_element_type=jnp.float32,
        )
        + proj_bias
    )
    parts = neighbours(received[..., :part_size], sec, 0).reshape(
        3, n_sp, n_rep, tok_frames, window, band_cols, out_width + 2
    )
    means = parts[..., out_width]
    mean = jnp.mean(means, axis=2)
    offsets = means - mean[:, :, None]
    m2 = jnp.sum(parts[..., out_width + 1], axis=2) + local_width * jnp.sum(
        offsets * offsets, axis=2
    )
    token_var = m2 / full_width
    centred_proj = jnp.sum(parts[..., :out_width], axis=2) + jnp.sum(
        offsets[..., None] * shard_columns.reshape(1, 1, n_rep, 1, 1, 1, out_width), axis=2
    )
    velocity = lax.rsqrt(token_var + 1e-06)[..., None] * centred_proj + shift_column
    patches = (
        velocity.reshape(3, frames, window, band_cols, LC, 2, 2)
        .transpose(1, 2, 5, 0, 3, 6, 4)
        .reshape(frames, 2 * window, 3 * 2 * band_cols, LC)
    )

    shares = neighbours(received[..., part_size:], sec, 0)
    if share == lines:
        shares = shares[:, :, 0]
    latent = shares.reshape(3, n_sp, frames, lat_cols, lat_rows, LC).transpose(0, 1, 2, 4, 3, 5)
    if window == patch_rows:
        latent = latent.transpose(2, 1, 3, 0, 4, 5).reshape(
            frames, n_sp * lat_rows, 3 * lat_cols, LC
        )
        clean = latent - 0.5 * patches
        clean = jnp.pad(clean, ((0, 0), (2, 2), (0, 0), (0, 0)))
        clean = lax.dynamic_slice_in_dim(clean, spi * lat_rows, lat_rows + 4, 1)
    else:
        latent = neighbours(latent.transpose(1, 2, 3, 0, 4, 5), spi, 0)
        latent = latent.transpose(1, 0, 2, 3, 4, 5).reshape(
            frames, 3 * lat_rows, 3 * lat_cols, LC
        )[:, lat_rows - 2 : 2 * lat_rows + 2]
        clean = latent - 0.5 * patches
    clean = clean[:, :, lat_cols - 2 : 2 * lat_cols + 2]

    row_global = spi * lat_rows - 2 + jnp.arange(lat_rows + 4)
    col_global = sec * lat_cols - 2 + jnp.arange(lat_cols + 4)
    row_inside = (row_global >= 0) & (row_global < lat_rows * n_sp)
    col_inside = (col_global >= 0) & (col_global < lat_cols * n_sec)
    clean = jnp.where(row_inside[None, :, None, None] & col_inside[None, None, :, None], clean, 0.0)

    inner_features = valid_conv(clean, in_weight, "DHWIO", lax.Precision.HIGH) + in_bias
    inside = row_inside[None, 1:-1, None, None] & col_inside[None, None, 1:-1, None]
    features = jnp.where(inside, inner_features, 0.0).astype(jnp.bfloat16)
    upsampled = jnp.repeat(jnp.repeat(features, 2, axis=1), 2, axis=2)[:, 1:-1, 1:-1, :]
    mixed = valid_conv(upsampled, conv_weight, "DHWOI", None) + conv_bias

    group_size = CO // GROUPS
    local_groups = mixed.shape[-1] // group_size
    grouped = mixed.reshape(-1, local_groups, group_size)
    block_count = grouped.shape[0] * group_size
    block_mean = jnp.sum(grouped, axis=(0, 2)) / block_count
    deviation = grouped - block_mean[None, :, None]
    block_m2 = jnp.sum(deviation * deviation, axis=(0, 2))
    n_blocks = n_sec * n_sp
    stats = jnp.broadcast_to(
        jnp.concatenate([block_mean, block_m2])[None], (n_blocks, 2 * local_groups)
    )
    stats = lax.all_to_all(stats, BLOCKS, 0, 0, tiled=False)
    group_mean = jnp.mean(stats[:, :local_groups], axis=0)
    mean_offsets = stats[:, :local_groups] - group_mean[None]
    group_var = (
        jnp.sum(stats[:, local_groups:], axis=0)
        + block_count * jnp.sum(mean_offsets * mean_offsets, axis=0)
    ) / (block_count * n_blocks)

    normed = (
        (grouped - group_mean[None, :, None]) * lax.rsqrt(group_var + 1e-06)[None, :, None]
    ).reshape(mixed.shape)
    activated = jax.nn.silu(normed * norm_gain + norm_bias)
    out_rows, out_cols, out_chan = (activated.shape[1], activated.shape[2], activated.shape[3])
    return activated.transpose(1, 2, 3, 0).reshape(out_rows, out_cols, out_chan * frames)


def solution(mesh):
    return jax.shard_map(
        per_device,
        mesh=mesh,
        in_specs=(
            P("sp", None, "section", "rep"),
            P(),
            P(),
            P(),
            P(),
            P(None, "sp", "section", None),
            P(),
            P(),
            P(None, None, None, "rep", None),
            P("rep"),
            P("rep"),
            P("rep"),
        ),
        out_specs=P("sp", "section", "rep"),
        check_vma=False,
    )
```

```python
import jax
import jax.numpy as jnp
from jax import lax
from jax.experimental import pallas as pl
from jax.experimental.pallas import tpu as pltpu
from jax.sharding import PartitionSpec as P

D = 3072
LC = 16
CO = 256
GROUPS = 32
ALL = ("section", "sp", "rep")
BLOCKS = ("section", "sp")


def valid_conv(volume, kernel, kernel_spec, precision_mode):
    front = jnp.concatenate([volume[:1], volume[:1], volume], axis=0)
    result = lax.conv_general_dilated(
        front[None],
        kernel,
        (1, 1, 1),
        "VALID",
        dimension_numbers=("NDHWC", kernel_spec, "NDHWC"),
        precision=precision_mode,
        preferred_element_type=jnp.float32,
    )
    return result[0]


def shard_kernel(rep_ref, tok_ref, weight_ref, scale_ref, out_ref):
    weight = weight_ref[...] * (1.0 + scale_ref[...])
    for frame in range(tok_ref.shape[0]):
        for row in range(tok_ref.shape[2]):
            x = tok_ref[frame, :, row, :]
            mean = jnp.mean(x, axis=1, keepdims=True)
            centred = x - mean
            width = weight.shape[0]
            out_ref[frame, row, :, :width] = lax.dot_general(
                centred,
                weight,
                (((1,), (1,)), ((), ())),
                precision=lax.Precision.HIGHEST,
                preferred_element_type=jnp.float32,
            )
            out_ref[frame, row, :, width : width + 1] = mean
            out_ref[frame, row, :, width + 1 : width + 2] = jnp.sum(
                centred * centred, axis=1, keepdims=True
            )


def shard_moments(tokens, proj_weight, mod_scale, rep):
    tok_frames, patch_rows, band_cols, local_width = tokens.shape
    out_width = proj_weight.shape[0]
    whole = lambda i, r: (0, 0, 0, 0)
    lead = (tok_frames, patch_rows, band_cols)
    return pl.pallas_call(
        shard_kernel,
        grid_spec=pltpu.PrefetchScalarGridSpec(
            num_scalar_prefetch=1,
            grid=(1,),
            in_specs=[
                pl.BlockSpec((tok_frames, band_cols, patch_rows, local_width), whole),
                pl.BlockSpec((out_width, local_width), lambda i, r: (0, r[0])),
                pl.BlockSpec((1, local_width), lambda i, r: (0, r[0])),
            ],
            out_specs=pl.BlockSpec(lead + (out_width + 2,), whole),
        ),
        out_shape=jax.ShapeDtypeStruct(lead + (out_width + 2,), jnp.float32),
    )(
        rep.reshape(1).astype(jnp.int32),
        tokens.transpose(0, 2, 1, 3),
        proj_weight,
        mod_scale.reshape(1, -1),
    )


def neighbours(stack, index, axis):
    pad = [(0, 0)] * stack.ndim
    pad[axis] = (1, 1)
    return lax.dynamic_slice_in_dim(jnp.pad(stack, pad), index, 3, axis)


def per_device(
    tokens,
    mod_scale,
    mod_shift,
    proj_weight,
    proj_bias,
    noisy_latent,
    in_weight,
    in_bias,
    conv_weight,
    conv_bias,
    norm_gain,
    norm_bias,
):
    n_sec, n_sp, n_rep = (lax.axis_size(a) for a in ALL)
    n_dev = n_sec * n_sp * n_rep
    sec, spi, rep = (lax.axis_index(a) for a in ALL)
    tok_frames, patch_rows, band_cols, local_width = tokens.shape
    frames, lat_rows, lat_cols, _ = noisy_latent.shape
    full_width = local_width * n_rep
    out_width = proj_weight.shape[0]

    partial = shard_moments(tokens, proj_weight, mod_scale, rep)

    slab = lat_rows // 2
    if patch_rows <= slab + 2:
        window = patch_rows
        per_slab = jnp.broadcast_to(partial[None], (n_sp,) + partial.shape)
    else:
        window = slab + 2
        padded = jnp.pad(partial, ((0, 0), (1, 1), (0, 0), (0, 0)))
        per_slab = jnp.stack([padded[:, p * slab : p * slab + window] for p in range(n_sp)])
    per_slab = per_slab.reshape(n_sp, -1)
    part_size = per_slab.shape[1]

    lines = frames * lat_cols
    stored = noisy_latent.transpose(0, 2, 1, 3).reshape(lines, lat_rows, LC)
    if lines % n_rep == 0:
        share = lines // n_rep
        latent_part = lax.dynamic_slice_in_dim(stored, rep * share, share, 0).reshape(-1)
    else:
        share = lines
        latent_part = stored.reshape(-1)

    send = jnp.concatenate(
        [
            jnp.broadcast_to(per_slab[None, :, None], (n_sec, n_sp, n_rep, part_size)),
            jnp.broadcast_to(latent_part, (n_sec, n_sp, n_rep, latent_part.shape[0])),
        ],
        axis=-1,
    ).reshape(n_dev, -1)
    received = lax.all_to_all(send, ALL, 0, 0, tiled=False).reshape(n_sec, n_sp, n_rep, -1)

    scaled_weight = proj_weight * (1.0 + mod_scale)[None, :]
    shard_columns = jnp.sum(scaled_weight.reshape(out_width, n_rep, local_width), axis=2).T
    shift_column = (
        jnp.dot(
            proj_weight,
            mod_shift,
            precision=lax.Precision.HIGHEST,
            preferred_element_type=jnp.float32,
        )
        + proj_bias
    )
    parts = neighbours(received[..., :part_size], sec, 0).reshape(
        3, n_sp, n_rep, tok_frames, window, band_cols, out_width + 2
    )
    means = parts[..., out_width]
    mean = jnp.mean(means, axis=2)
    offsets = means - mean[:, :, None]
    m2 = jnp.sum(parts[..., out_width + 1], axis=2) + local_width * jnp.sum(
        offsets * offsets, axis=2
    )
    token_var = m2 / full_width
    centred_proj = jnp.sum(parts[..., :out_width], axis=2) + lax.dot_general(
        offsets,
        shard_columns,
        (((2,), (0,)), ((), ())),
        precision=lax.Precision.HIGHEST,
        preferred_element_type=jnp.float32,
    )
    velocity = lax.rsqrt(token_var + 1e-06)[..., None] * centred_proj + shift_column
    patches = (
        velocity.reshape(3, frames, window, band_cols, LC, 2, 2)
        .transpose(1, 2, 5, 0, 3, 6, 4)
        .reshape(frames, 2 * window, 3 * 2 * band_cols, LC)
    )

    shares = neighbours(received[..., part_size:], sec, 0)
    if share == lines:
        shares = shares[:, :, 0]
    latent = shares.reshape(3, n_sp, frames, lat_cols, lat_rows, LC).transpose(0, 1, 2, 4, 3, 5)
    if window == patch_rows:
        latent = latent.transpose(2, 1, 3, 0, 4, 5).reshape(
            frames, n_sp * lat_rows, 3 * lat_cols, LC
        )
        clean = latent - 0.5 * patches
        clean = jnp.pad(clean, ((0, 0), (2, 2), (0, 0), (0, 0)))
        clean = lax.dynamic_slice_in_dim(clean, spi * lat_rows, lat_rows + 4, 1)
    else:
        latent = neighbours(latent.transpose(1, 2, 3, 0, 4, 5), spi, 0)
        latent = latent.transpose(1, 0, 2, 3, 4, 5).reshape(
            frames, 3 * lat_rows, 3 * lat_cols, LC
        )[:, lat_rows - 2 : 2 * lat_rows + 2]
        clean = latent - 0.5 * patches
    clean = clean[:, :, lat_cols - 2 : 2 * lat_cols + 2]

    row_global = spi * lat_rows - 2 + jnp.arange(lat_rows + 4)
    col_global = sec * lat_cols - 2 + jnp.arange(lat_cols + 4)
    row_inside = (row_global >= 0) & (row_global < lat_rows * n_sp)
    col_inside = (col_global >= 0) & (col_global < lat_cols * n_sec)
    clean = jnp.where(row_inside[None, :, None, None] & col_inside[None, None, :, None], clean, 0.0)

    front = jnp.concatenate([clean[:1], clean[:1], clean], axis=0)
    taps = jnp.concatenate(
        [
            front[dt : dt + frames, dy : dy + lat_rows + 2, dx : dx + lat_cols + 2]
            for dt in range(3)
            for dy in range(3)
            for dx in range(3)
        ],
        axis=-1,
    )
    inner_features = (
        lax.dot_general(
            taps,
            in_weight.reshape(-1, in_weight.shape[-1]),
            (((3,), (0,)), ((), ())),
            precision=lax.Precision.HIGH,
            preferred_element_type=jnp.float32,
        )
        + in_bias
    )
    inside = row_inside[None, 1:-1, None, None] & col_inside[None, None, 1:-1, None]
    features = jnp.where(inside, inner_features, 0.0).astype(jnp.bfloat16)
    upsampled = jnp.repeat(jnp.repeat(features, 2, axis=1), 2, axis=2)[:, 1:-1, 1:-1, :]
    mixed = valid_conv(upsampled, conv_weight, "DHWOI", None) + conv_bias

    group_size = CO // GROUPS
    local_groups = mixed.shape[-1] // group_size
    grouped = mixed.reshape(-1, local_groups, group_size)
    block_count = grouped.shape[0] * group_size
    block_mean = jnp.sum(grouped, axis=(0, 2)) / block_count
    deviation = grouped - block_mean[None, :, None]
    block_m2 = jnp.sum(deviation * deviation, axis=(0, 2))
    n_blocks = n_sec * n_sp
    stats = jnp.broadcast_to(
        jnp.concatenate([block_mean, block_m2])[None], (n_blocks, 2 * local_groups)
    )
    stats = lax.all_to_all(stats, BLOCKS, 0, 0, tiled=False)
    group_mean = jnp.mean(stats[:, :local_groups], axis=0)
    mean_offsets = stats[:, :local_groups] - group_mean[None]
    group_var = (
        jnp.sum(stats[:, local_groups:], axis=0)
        + block_count * jnp.sum(mean_offsets * mean_offsets, axis=0)
    ) / (block_count * n_blocks)

    normed = (
        (grouped - group_mean[None, :, None]) * lax.rsqrt(group_var + 1e-06)[None, :, None]
    ).reshape(mixed.shape)
    activated = jax.nn.silu(normed * norm_gain + norm_bias)
    out_rows, out_cols, out_chan = (activated.shape[1], activated.shape[2], activated.shape[3])
    return activated.transpose(1, 2, 3, 0).reshape(out_rows, out_cols, out_chan * frames)


def solution(mesh):
    return jax.shard_map(
        per_device,
        mesh=mesh,
        in_specs=(
            P("sp", None, "section", "rep"),
            P(),
            P(),
            P(),
            P(),
            P(None, "sp", "section", None),
            P(),
            P(),
            P(None, None, None, "rep", None),
            P("rep"),
            P("rep"),
            P("rep"),
        ),
        out_specs=P("sp", "section", "rep"),
        check_vma=False,
    )
```

```python
import jax
import jax.numpy as jnp
from jax import lax
from jax.experimental import pallas as pl
from jax.experimental.pallas import tpu as pltpu
from jax.sharding import PartitionSpec as P

D = 3072
LC = 16
CO = 256
GROUPS = 32
ALL = ("section", "sp", "rep")
BLOCKS = ("section", "sp")


def valid_conv(volume, kernel, kernel_spec, precision_mode):
    front = jnp.concatenate([volume[:1], volume[:1], volume], axis=0)
    result = lax.conv_general_dilated(
        front[None],
        kernel,
        (1, 1, 1),
        "VALID",
        dimension_numbers=("NDHWC", kernel_spec, "NDHWC"),
        precision=precision_mode,
        preferred_element_type=jnp.float32,
    )
    return result[0]


def shard_kernel(rep_ref, tok_ref, weight_ref, scale_ref, out_ref):
    weight = weight_ref[...] * (1.0 + scale_ref[...])
    for frame in range(tok_ref.shape[0]):
        for row in range(tok_ref.shape[2]):
            x = tok_ref[frame, :, row, :]
            mean = jnp.mean(x, axis=1, keepdims=True)
            centred = x - mean
            width = weight.shape[0]
            out_ref[frame, row, :, :width] = lax.dot_general(
                centred,
                weight,
                (((1,), (1,)), ((), ())),
                precision=lax.Precision.HIGHEST,
                preferred_element_type=jnp.float32,
            )
            out_ref[frame, row, :, width : width + 1] = mean
            out_ref[frame, row, :, width + 1 : width + 2] = jnp.sum(
                centred * centred, axis=1, keepdims=True
            )


def shard_moments(tokens, proj_weight, mod_scale, rep):
    tok_frames, patch_rows, band_cols, local_width = tokens.shape
    out_width = proj_weight.shape[0]
    whole = lambda i, r: (0, 0, 0, 0)
    lead = (tok_frames, patch_rows, band_cols)
    return pl.pallas_call(
        shard_kernel,
        grid_spec=pltpu.PrefetchScalarGridSpec(
            num_scalar_prefetch=1,
            grid=(1,),
            in_specs=[
                pl.BlockSpec((tok_frames, band_cols, patch_rows, local_width), whole),
                pl.BlockSpec((out_width, local_width), lambda i, r: (0, r[0])),
                pl.BlockSpec((1, local_width), lambda i, r: (0, r[0])),
            ],
            out_specs=pl.BlockSpec(lead + (out_width + 2,), whole),
        ),
        out_shape=jax.ShapeDtypeStruct(lead + (out_width + 2,), jnp.float32),
    )(
        rep.reshape(1).astype(jnp.int32),
        tokens.transpose(0, 2, 1, 3),
        proj_weight,
        mod_scale.reshape(1, -1),
    )


def neighbours(stack, index, axis):
    pad = [(0, 0)] * stack.ndim
    pad[axis] = (1, 1)
    return lax.dynamic_slice_in_dim(jnp.pad(stack, pad), index, 3, axis)


def per_device(
    tokens,
    mod_scale,
    mod_shift,
    proj_weight,
    proj_bias,
    noisy_latent,
    in_weight,
    in_bias,
    conv_weight,
    conv_bias,
    norm_gain,
    norm_bias,
):
    n_sec, n_sp, n_rep = (lax.axis_size(a) for a in ALL)
    n_dev = n_sec * n_sp * n_rep
    sec, spi, rep = (lax.axis_index(a) for a in ALL)
    tok_frames, patch_rows, band_cols, local_width = tokens.shape
    frames, lat_rows, lat_cols, _ = noisy_latent.shape
    full_width = local_width * n_rep
    out_width = proj_weight.shape[0]

    partial = shard_moments(tokens, proj_weight, mod_scale, rep)

    slab = lat_rows // 2
    if patch_rows <= slab + 2:
        window = patch_rows
        per_slab = jnp.broadcast_to(partial[None], (n_sp,) + partial.shape)
    else:
        window = slab + 2
        padded = jnp.pad(partial, ((0, 0), (1, 1), (0, 0), (0, 0)))
        per_slab = jnp.stack([padded[:, p * slab : p * slab + window] for p in range(n_sp)])
    per_slab = per_slab.reshape(n_sp, -1)
    part_size = per_slab.shape[1]

    lines = frames * lat_cols
    stored = noisy_latent.transpose(0, 2, 1, 3).reshape(lines, lat_rows, LC)
    if lines % n_rep == 0:
        share = lines // n_rep
        latent_part = lax.dynamic_slice_in_dim(stored, rep * share, share, 0).reshape(-1)
    else:
        share = lines
        latent_part = stored.reshape(-1)

    send = jnp.concatenate(
        [
            jnp.broadcast_to(per_slab[None, :, None], (n_sec, n_sp, n_rep, part_size)),
            jnp.broadcast_to(latent_part, (n_sec, n_sp, n_rep, latent_part.shape[0])),
        ],
        axis=-1,
    ).reshape(n_dev, -1)
    received = lax.all_to_all(send, ALL, 0, 0, tiled=False).reshape(n_sec, n_sp, n_rep, -1)

    scaled_weight = proj_weight * (1.0 + mod_scale)[None, :]
    shard_columns = jnp.sum(scaled_weight.reshape(out_width, n_rep, local_width), axis=2).T
    shift_column = (
        jnp.dot(
            proj_weight,
            mod_shift,
            precision=lax.Precision.HIGHEST,
            preferred_element_type=jnp.float32,
        )
        + proj_bias
    )
    parts = neighbours(received[..., :part_size], sec, 0).reshape(
        3, n_sp, n_rep, tok_frames, window, band_cols, out_width + 2
    )
    means = parts[..., out_width]
    mean = jnp.mean(means, axis=2)
    offsets = means - mean[:, :, None]
    m2 = jnp.sum(parts[..., out_width + 1], axis=2) + local_width * jnp.sum(
        offsets * offsets, axis=2
    )
    token_var = m2 / full_width
    centred_proj = jnp.sum(parts[..., :out_width], axis=2) + lax.dot_general(
        offsets,
        shard_columns,
        (((2,), (0,)), ((), ())),
        precision=lax.Precision.HIGHEST,
        preferred_element_type=jnp.float32,
    )
    velocity = lax.rsqrt(token_var + 1e-06)[..., None] * centred_proj + shift_column
    patches = (
        velocity.reshape(3, frames, window, band_cols, LC, 2, 2)
        .transpose(1, 2, 5, 0, 3, 6, 4)
        .reshape(frames, 2 * window, 3 * 2 * band_cols, LC)
    )

    shares = neighbours(received[..., part_size:], sec, 0)
    if share == lines:
        shares = shares[:, :, 0]
    latent = shares.reshape(3, n_sp, frames, lat_cols, lat_rows, LC).transpose(0, 1, 2, 4, 3, 5)
    if window == patch_rows:
        latent = latent.transpose(2, 1, 3, 0, 4, 5).reshape(
            frames, n_sp * lat_rows, 3 * lat_cols, LC
        )
        clean = latent - 0.5 * patches
        clean = jnp.pad(clean, ((0, 0), (2, 2), (0, 0), (0, 0)))
        clean = lax.dynamic_slice_in_dim(clean, spi * lat_rows, lat_rows + 4, 1)
    else:
        latent = neighbours(latent.transpose(1, 2, 3, 0, 4, 5), spi, 0)
        latent = latent.transpose(1, 0, 2, 3, 4, 5).reshape(
            frames, 3 * lat_rows, 3 * lat_cols, LC
        )[:, lat_rows - 2 : 2 * lat_rows + 2]
        clean = latent - 0.5 * patches
    clean = clean[:, :, lat_cols - 2 : 2 * lat_cols + 2]

    row_global = spi * lat_rows - 2 + jnp.arange(lat_rows + 4)
    col_global = sec * lat_cols - 2 + jnp.arange(lat_cols + 4)
    row_inside = (row_global >= 0) & (row_global < lat_rows * n_sp)
    col_inside = (col_global >= 0) & (col_global < lat_cols * n_sec)
    clean = jnp.where(row_inside[None, :, None, None] & col_inside[None, None, :, None], clean, 0.0)

    inner_features = valid_conv(clean, in_weight, "DHWIO", lax.Precision.HIGH) + in_bias
    inside = row_inside[None, 1:-1, None, None] & col_inside[None, None, 1:-1, None]
    features = jnp.where(inside, inner_features, 0.0).astype(jnp.bfloat16)
    upsampled = jnp.repeat(jnp.repeat(features, 2, axis=1), 2, axis=2)[:, 1:-1, 1:-1, :]
    mixed = valid_conv(upsampled, conv_weight, "DHWOI", None) + conv_bias

    group_size = CO // GROUPS
    local_groups = mixed.shape[-1] // group_size
    grouped = mixed.reshape(-1, local_groups, group_size)
    block_count = grouped.shape[0] * group_size
    block_mean = jnp.sum(grouped, axis=(0, 2)) / block_count
    deviation = grouped - block_mean[None, :, None]
    block_m2 = jnp.sum(deviation * deviation, axis=(0, 2))
    n_blocks = n_sec * n_sp
    stats = jnp.broadcast_to(
        jnp.concatenate([block_mean, block_m2])[None], (n_blocks, 2 * local_groups)
    )
    stats = lax.all_to_all(stats, BLOCKS, 0, 0, tiled=False)
    group_mean = jnp.mean(stats[:, :local_groups], axis=0)
    mean_offsets = stats[:, :local_groups] - group_mean[None]
    group_var = (
        jnp.sum(stats[:, local_groups:], axis=0)
        + block_count * jnp.sum(mean_offsets * mean_offsets, axis=0)
    ) / (block_count * n_blocks)

    normed = (
        (grouped - group_mean[None, :, None]) * lax.rsqrt(group_var + 1e-06)[None, :, None]
    ).reshape(mixed.shape)
    activated = jax.nn.silu(normed * norm_gain + norm_bias)
    out_rows, out_cols, out_chan = (activated.shape[1], activated.shape[2], activated.shape[3])
    return activated.transpose(1, 2, 3, 0).reshape(out_rows, out_cols, out_chan * frames)


def solution(mesh):
    return jax.shard_map(
        per_device,
        mesh=mesh,
        in_specs=(
            P("sp", None, "section", "rep"),
            P(),
            P(),
            P(),
            P(),
            P(None, "sp", "section", None),
            P(),
            P(),
            P(None, None, None, "rep", None),
            P("rep"),
            P("rep"),
            P("rep"),
        ),
        out_specs=P("sp", "section", "rep"),
        check_vma=False,
    )
```

```python
import jax
import jax.numpy as jnp
from jax import lax
from jax.experimental import pallas as pl
from jax.experimental.pallas import tpu as pltpu
from jax.sharding import PartitionSpec as P

D = 3072
LC = 16
CO = 256
GROUPS = 32
ALL = ("section", "sp", "rep")
BLOCKS = ("section", "sp")


def causal_front(volume):
    return jnp.concatenate([volume[:1], volume[:1], volume], axis=0)


def valid_conv(front, kernel, kernel_spec, precision_mode):
    result = lax.conv_general_dilated(
        front[None],
        kernel,
        (1, 1, 1),
        "VALID",
        dimension_numbers=("NDHWC", kernel_spec, "NDHWC"),
        precision=precision_mode,
        preferred_element_type=jnp.float32,
    )
    return result[0]


def shard_kernel(rep_ref, tok_ref, weight_ref, scale_ref, latent_ref, out_ref, share_ref):
    share_ref[...] = latent_ref[...]
    weight = weight_ref[...] * (1.0 + scale_ref[...])
    for frame in range(tok_ref.shape[0]):
        for row in range(tok_ref.shape[2]):
            x = tok_ref[frame, :, row, :]
            mean = jnp.mean(x, axis=1, keepdims=True)
            centred = x - mean
            width = weight.shape[0]
            out_ref[frame, row, :, :width] = lax.dot_general(
                centred,
                weight,
                (((1,), (1,)), ((), ())),
                precision=lax.Precision.HIGHEST,
                preferred_element_type=jnp.float32,
            )
            out_ref[frame, row, :, width : width + 1] = mean
            out_ref[frame, row, :, width + 1 : width + 2] = jnp.sum(
                centred * centred, axis=1, keepdims=True
            )


def shard_moments(tokens, proj_weight, mod_scale, latent_lines, share, rep):
    tok_frames, patch_rows, band_cols, local_width = tokens.shape
    out_width = proj_weight.shape[0]
    whole = lambda i, r: (0, 0, 0, 0)
    whole3 = lambda i, r: (0, 0, 0)
    lead = (tok_frames, patch_rows, band_cols)
    return pl.pallas_call(
        shard_kernel,
        grid_spec=pltpu.PrefetchScalarGridSpec(
            num_scalar_prefetch=1,
            grid=(1,),
            in_specs=[
                pl.BlockSpec((tok_frames, band_cols, patch_rows, local_width), whole),
                pl.BlockSpec((out_width, local_width), lambda i, r: (0, r[0])),
                pl.BlockSpec((1, local_width), lambda i, r: (0, r[0])),
                pl.BlockSpec(
                    (share,) + latent_lines.shape[1:],
                    (lambda i, r: (r[0], 0, 0)) if share < latent_lines.shape[0] else whole3,
                ),
            ],
            out_specs=[
                pl.BlockSpec(lead + (out_width + 2,), whole),
                pl.BlockSpec((share,) + latent_lines.shape[1:], whole3),
            ],
        ),
        out_shape=[
            jax.ShapeDtypeStruct(lead + (out_width + 2,), jnp.float32),
            jax.ShapeDtypeStruct((share,) + latent_lines.shape[1:], jnp.float32),
        ],
    )(
        rep.reshape(1).astype(jnp.int32),
        tokens.transpose(0, 2, 1, 3),
        proj_weight,
        mod_scale.reshape(1, -1),
        latent_lines,
    )


def neighbours(stack, index, axis):
    pad = [(0, 0)] * stack.ndim
    pad[axis] = (1, 1)
    return lax.dynamic_slice_in_dim(jnp.pad(stack, pad), index, 3, axis)


def per_device(
    tokens,
    mod_scale,
    mod_shift,
    proj_weight,
    proj_bias,
    noisy_latent,
    in_weight,
    in_bias,
    conv_weight,
    conv_bias,
    norm_gain,
    norm_bias,
):
    n_sec, n_sp, n_rep = (lax.axis_size(a) for a in ALL)
    n_dev = n_sec * n_sp * n_rep
    sec, spi, rep = (lax.axis_index(a) for a in ALL)
    tok_frames, patch_rows, band_cols, local_width = tokens.shape
    frames, lat_rows, lat_cols, _ = noisy_latent.shape
    full_width = local_width * n_rep
    out_width = proj_weight.shape[0]


    lines = frames * lat_cols
    stored = noisy_latent.transpose(0, 2, 1, 3).reshape(lines, lat_rows, LC)
    share = lines // n_rep if lines % n_rep == 0 else lines
    partial, latent_part = shard_moments(
        tokens, proj_weight, mod_scale, stored, share, rep
    )
    latent_part = latent_part.reshape(-1)

    slab = lat_rows // 2
    if patch_rows <= slab + 2:
        window = patch_rows
        per_slab = jnp.broadcast_to(partial[None], (n_sp,) + partial.shape)
    else:
        window = slab + 2
        padded = jnp.pad(partial, ((0, 0), (1, 1), (0, 0), (0, 0)))
        per_slab = jnp.stack([padded[:, p * slab : p * slab + window] for p in range(n_sp)])
    per_slab = per_slab.reshape(n_sp, -1)
    part_size = per_slab.shape[1]

    send = jnp.concatenate(
        [
            jnp.broadcast_to(per_slab[None, :, None], (n_sec, n_sp, n_rep, part_size)),
            jnp.broadcast_to(latent_part, (n_sec, n_sp, n_rep, latent_part.shape[0])),
        ],
        axis=-1,
    ).reshape(n_dev, -1)
    received = lax.all_to_all(send, ALL, 0, 0, tiled=False).reshape(n_sec, n_sp, n_rep, -1)

    scaled_weight = proj_weight * (1.0 + mod_scale)[None, :]
    shard_columns = jnp.sum(scaled_weight.reshape(out_width, n_rep, local_width), axis=2).T
    shift_column = (
        jnp.dot(
            proj_weight,
            mod_shift,
            precision=lax.Precision.HIGHEST,
            preferred_element_type=jnp.float32,
        )
        + proj_bias
    )
    parts = neighbours(received[..., :part_size], sec, 0).reshape(
        3, n_sp, n_rep, tok_frames, window, band_cols, out_width + 2
    )
    means = parts[..., out_width]
    mean = jnp.mean(means, axis=2)
    offsets = means - mean[:, :, None]
    m2 = jnp.sum(parts[..., out_width + 1], axis=2) + local_width * jnp.sum(
        offsets * offsets, axis=2
    )
    token_var = m2 / full_width
    centred_proj = jnp.sum(parts[..., :out_width], axis=2) + lax.dot_general(
        offsets,
        shard_columns,
        (((2,), (0,)), ((), ())),
        precision=lax.Precision.HIGHEST,
        preferred_element_type=jnp.float32,
    )
    velocity = lax.rsqrt(token_var + 1e-06)[..., None] * centred_proj + shift_column
    patches = (
        velocity.reshape(3, frames, window, band_cols, LC, 2, 2)
        .transpose(1, 2, 5, 0, 3, 6, 4)
        .reshape(frames, 2 * window, 3 * 2 * band_cols, LC)
    )

    shares = neighbours(received[..., part_size:], sec, 0)
    if share == lines:
        shares = shares[:, :, 0]
    latent = shares.reshape(3, n_sp, frames, lat_cols, lat_rows, LC).transpose(0, 1, 2, 4, 3, 5)
    if window == patch_rows:
        latent = latent.transpose(2, 1, 3, 0, 4, 5).reshape(
            frames, n_sp * lat_rows, 3 * lat_cols, LC
        )
        clean = latent - 0.5 * patches
        clean = jnp.pad(clean, ((0, 0), (2, 2), (0, 0), (0, 0)))
        clean = lax.dynamic_slice_in_dim(clean, spi * lat_rows, lat_rows + 4, 1)
    else:
        latent = neighbours(latent.transpose(1, 2, 3, 0, 4, 5), spi, 0)
        latent = latent.transpose(1, 0, 2, 3, 4, 5).reshape(
            frames, 3 * lat_rows, 3 * lat_cols, LC
        )[:, lat_rows - 2 : 2 * lat_rows + 2]
        clean = latent - 0.5 * patches
    clean = clean[:, :, lat_cols - 2 : 2 * lat_cols + 2]

    row_global = spi * lat_rows - 2 + jnp.arange(lat_rows + 4)
    col_global = sec * lat_cols - 2 + jnp.arange(lat_cols + 4)
    row_inside = (row_global >= 0) & (row_global < lat_rows * n_sp)
    col_inside = (col_global >= 0) & (col_global < lat_cols * n_sec)
    clean = jnp.where(row_inside[None, :, None, None] & col_inside[None, None, :, None], clean, 0.0)

    inner_features = valid_conv(causal_front(clean), in_weight, "DHWIO", lax.Precision.HIGH) + in_bias
    inside = row_inside[None, 1:-1, None, None] & col_inside[None, None, 1:-1, None]
    features = causal_front(jnp.where(inside, inner_features, 0.0).astype(jnp.bfloat16))
    upsampled = jnp.repeat(jnp.repeat(features, 2, axis=1), 2, axis=2)[:, 1:-1, 1:-1, :]
    mixed = valid_conv(upsampled, conv_weight, "DHWOI", None) + conv_bias

    group_size = CO // GROUPS
    local_groups = mixed.shape[-1] // group_size
    grouped = mixed.reshape(-1, local_groups, group_size)
    block_count = grouped.shape[0] * group_size
    block_mean = jnp.sum(grouped, axis=(0, 2)) / block_count
    deviation = grouped - block_mean[None, :, None]
    block_m2 = jnp.sum(deviation * deviation, axis=(0, 2))
    n_blocks = n_sec * n_sp
    stats = jnp.broadcast_to(
        jnp.concatenate([block_mean, block_m2])[None], (n_blocks, 2 * local_groups)
    )
    stats = lax.all_to_all(stats, BLOCKS, 0, 0, tiled=False)
    group_mean = jnp.mean(stats[:, :local_groups], axis=0)
    mean_offsets = stats[:, :local_groups] - group_mean[None]
    group_var = (
        jnp.sum(stats[:, local_groups:], axis=0)
        + block_count * jnp.sum(mean_offsets * mean_offsets, axis=0)
    ) / (block_count * n_blocks)

    normed = (
        (grouped - group_mean[None, :, None]) * lax.rsqrt(group_var + 1e-06)[None, :, None]
    ).reshape(mixed.shape)
    activated = jax.nn.silu(normed * norm_gain + norm_bias)
    out_rows, out_cols, out_chan = (activated.shape[1], activated.shape[2], activated.shape[3])
    return activated.transpose(1, 2, 3, 0).reshape(out_rows, out_cols, out_chan * frames)


def solution(mesh):
    return jax.shard_map(
        per_device,
        mesh=mesh,
        in_specs=(
            P("sp", None, "section", "rep"),
            P(),
            P(),
            P(),
            P(),
            P(None, "sp", "section", None),
            P(),
            P(),
            P(None, None, None, "rep", None),
            P("rep"),
            P("rep"),
            P("rep"),
        ),
        out_specs=P("sp", "section", "rep"),
        check_vma=False,
    )
```

```python
import jax
import jax.numpy as jnp
from jax import lax
from jax.experimental import pallas as pl
from jax.experimental.pallas import tpu as pltpu
from jax.sharding import PartitionSpec as P

D = 3072
LC = 16
CO = 256
GROUPS = 32
ALL = ("section", "sp", "rep")
BLOCKS = ("section", "sp")


def causal_front(volume):
    return jnp.concatenate([volume[:1], volume[:1], volume], axis=0)


def valid_conv(front, kernel, kernel_spec, precision_mode):
    result = lax.conv_general_dilated(
        front[None],
        kernel,
        (1, 1, 1),
        "VALID",
        dimension_numbers=("NDHWC", kernel_spec, "NDHWC"),
        precision=precision_mode,
        preferred_element_type=jnp.float32,
    )
    return result[0]


def shard_kernel(rep_ref, tok_ref, weight_ref, scale_ref, latent_ref, out_ref):
    weight = weight_ref[...] * (1.0 + scale_ref[...])
    width = weight.shape[0]
    band_cols = tok_ref.shape[1]
    record = width + 2
    for frame in range(tok_ref.shape[0]):
        for row in range(tok_ref.shape[2]):
            x = tok_ref[frame, :, row, :]
            mean = jnp.mean(x, axis=1, keepdims=True)
            centred = x - mean
            m2 = jnp.sum(centred * centred, axis=1, keepdims=True)
            projected = lax.dot_general(
                centred,
                weight,
                (((1,), (1,)), ((), ())),
                precision=lax.Precision.HIGHEST,
                preferred_element_type=jnp.float32,
            )
            for col in range(band_cols):
                base = ((frame * tok_ref.shape[2] + row) * band_cols + col) * record
                out_ref[:, pl.ds(base, width)] = projected[col : col + 1, :]
                out_ref[:, pl.ds(base + width, 1)] = mean[col : col + 1, :]
                out_ref[:, pl.ds(base + width + 1, 1)] = m2[col : col + 1, :]
    lines, lat_rows, channels = latent_ref.shape
    offset = tok_ref.shape[0] * tok_ref.shape[2] * band_cols * record
    share = latent_ref[...]
    for line in range(lines):
        for row in range(lat_rows):
            out_ref[:, pl.ds(offset + (line * lat_rows + row) * channels, channels)] = share[
                line, row : row + 1, :
            ]


def shard_moments(tokens, proj_weight, mod_scale, latent_lines, share, rep):
    tok_frames, patch_rows, band_cols, local_width = tokens.shape
    out_width = proj_weight.shape[0]
    size = tok_frames * patch_rows * band_cols * (out_width + 2) + latent_lines[0].size * share
    whole = lambda i, r: (0, 0, 0, 0)
    whole3 = lambda i, r: (0, 0, 0)
    return pl.pallas_call(
        shard_kernel,
        grid_spec=pltpu.PrefetchScalarGridSpec(
            num_scalar_prefetch=1,
            grid=(1,),
            in_specs=[
                pl.BlockSpec((tok_frames, band_cols, patch_rows, local_width), whole),
                pl.BlockSpec((out_width, local_width), lambda i, r: (0, r[0])),
                pl.BlockSpec((1, local_width), lambda i, r: (0, r[0])),
                pl.BlockSpec(
                    (share,) + latent_lines.shape[1:],
                    (lambda i, r: (r[0], 0, 0)) if share < latent_lines.shape[0] else whole3,
                ),
            ],
            out_specs=pl.BlockSpec((1, size), lambda i, r: (0, 0)),
        ),
        out_shape=jax.ShapeDtypeStruct((1, size), jnp.float32),
    )(
        rep.reshape(1).astype(jnp.int32),
        tokens.transpose(0, 2, 1, 3),
        proj_weight,
        mod_scale.reshape(1, -1),
        latent_lines,
    )[0]


def neighbours(stack, index, axis):
    pad = [(0, 0)] * stack.ndim
    pad[axis] = (1, 1)
    return lax.dynamic_slice_in_dim(jnp.pad(stack, pad), index, 3, axis)


def per_device(
    tokens,
    mod_scale,
    mod_shift,
    proj_weight,
    proj_bias,
    noisy_latent,
    in_weight,
    in_bias,
    conv_weight,
    conv_bias,
    norm_gain,
    norm_bias,
):
    n_sec, n_sp, n_rep = (lax.axis_size(a) for a in ALL)
    n_dev = n_sec * n_sp * n_rep
    sec, spi, rep = (lax.axis_index(a) for a in ALL)
    tok_frames, patch_rows, band_cols, local_width = tokens.shape
    frames, lat_rows, lat_cols, _ = noisy_latent.shape
    full_width = local_width * n_rep
    out_width = proj_weight.shape[0]


    lines = frames * lat_cols
    stored = noisy_latent.transpose(0, 2, 1, 3).reshape(lines, lat_rows, LC)
    share = lines // n_rep if lines % n_rep == 0 else lines
    payload = shard_moments(tokens, proj_weight, mod_scale, stored, share, rep)
    part_flat = tok_frames * patch_rows * band_cols * (out_width + 2)

    slab = lat_rows // 2
    if patch_rows <= slab + 2:
        window = patch_rows
        part_size = part_flat
        send = jnp.broadcast_to(payload, (n_dev, payload.shape[0]))
    else:
        window = slab + 2
        partial = payload[:part_flat].reshape(tok_frames, patch_rows, band_cols, out_width + 2)
        padded = jnp.pad(partial, ((0, 0), (1, 1), (0, 0), (0, 0)))
        per_slab = jnp.stack([padded[:, p * slab : p * slab + window] for p in range(n_sp)])
        per_slab = per_slab.reshape(n_sp, -1)
        part_size = per_slab.shape[1]
        latent_part = payload[part_flat:]
        send = jnp.concatenate(
            [
                jnp.broadcast_to(per_slab[None, :, None], (n_sec, n_sp, n_rep, part_size)),
                jnp.broadcast_to(latent_part, (n_sec, n_sp, n_rep, latent_part.shape[0])),
            ],
            axis=-1,
        ).reshape(n_dev, -1)
    received = lax.all_to_all(send, ALL, 0, 0, tiled=False).reshape(n_sec, n_sp, n_rep, -1)

    scaled_weight = proj_weight * (1.0 + mod_scale)[None, :]
    shard_columns = jnp.sum(scaled_weight.reshape(out_width, n_rep, local_width), axis=2).T
    shift_column = (
        jnp.dot(
            proj_weight,
            mod_shift,
            precision=lax.Precision.HIGHEST,
            preferred_element_type=jnp.float32,
        )
        + proj_bias
    )
    parts = neighbours(received[..., :part_size], sec, 0).reshape(
        3, n_sp, n_rep, tok_frames, window, band_cols, out_width + 2
    )
    means = parts[..., out_width]
    mean = jnp.mean(means, axis=2)
    offsets = means - mean[:, :, None]
    m2 = jnp.sum(parts[..., out_width + 1], axis=2) + local_width * jnp.sum(
        offsets * offsets, axis=2
    )
    token_var = m2 / full_width
    centred_proj = jnp.sum(parts[..., :out_width], axis=2) + lax.dot_general(
        offsets,
        shard_columns,
        (((2,), (0,)), ((), ())),
        precision=lax.Precision.HIGHEST,
        preferred_element_type=jnp.float32,
    )
    velocity = lax.rsqrt(token_var + 1e-06)[..., None] * centred_proj + shift_column
    patches = (
        velocity.reshape(3, frames, window, band_cols, LC, 2, 2)
        .transpose(1, 2, 5, 0, 3, 6, 4)
        .reshape(frames, 2 * window, 3 * 2 * band_cols, LC)
    )

    shares = neighbours(received[..., part_size:], sec, 0)
    if share == lines:
        shares = shares[:, :, 0]
    latent = shares.reshape(3, n_sp, frames, lat_cols, lat_rows, LC).transpose(0, 1, 2, 4, 3, 5)
    if window == patch_rows:
        latent = latent.transpose(2, 1, 3, 0, 4, 5).reshape(
            frames, n_sp * lat_rows, 3 * lat_cols, LC
        )
        clean = latent - 0.5 * patches
        clean = jnp.pad(clean, ((0, 0), (2, 2), (0, 0), (0, 0)))
        clean = lax.dynamic_slice_in_dim(clean, spi * lat_rows, lat_rows + 4, 1)
    else:
        latent = neighbours(latent.transpose(1, 2, 3, 0, 4, 5), spi, 0)
        latent = latent.transpose(1, 0, 2, 3, 4, 5).reshape(
            frames, 3 * lat_rows, 3 * lat_cols, LC
        )[:, lat_rows - 2 : 2 * lat_rows + 2]
        clean = latent - 0.5 * patches
    clean = clean[:, :, lat_cols - 2 : 2 * lat_cols + 2]

    row_global = spi * lat_rows - 2 + jnp.arange(lat_rows + 4)
    col_global = sec * lat_cols - 2 + jnp.arange(lat_cols + 4)
    row_inside = (row_global >= 0) & (row_global < lat_rows * n_sp)
    col_inside = (col_global >= 0) & (col_global < lat_cols * n_sec)
    clean = jnp.where(row_inside[None, :, None, None] & col_inside[None, None, :, None], clean, 0.0)

    inner_features = valid_conv(causal_front(clean), in_weight, "DHWIO", lax.Precision.HIGH) + in_bias
    inside = row_inside[None, 1:-1, None, None] & col_inside[None, None, 1:-1, None]
    features = causal_front(jnp.where(inside, inner_features, 0.0).astype(jnp.bfloat16))
    upsampled = jnp.repeat(jnp.repeat(features, 2, axis=1), 2, axis=2)[:, 1:-1, 1:-1, :]
    mixed = valid_conv(upsampled, conv_weight, "DHWOI", None) + conv_bias

    group_size = CO // GROUPS
    local_groups = mixed.shape[-1] // group_size
    grouped = mixed.reshape(-1, local_groups, group_size)
    block_count = grouped.shape[0] * group_size
    block_mean = jnp.sum(grouped, axis=(0, 2)) / block_count
    deviation = grouped - block_mean[None, :, None]
    block_m2 = jnp.sum(deviation * deviation, axis=(0, 2))
    n_blocks = n_sec * n_sp
    stats = jnp.broadcast_to(
        jnp.concatenate([block_mean, block_m2])[None], (n_blocks, 2 * local_groups)
    )
    stats = lax.all_to_all(stats, BLOCKS, 0, 0, tiled=False)
    group_mean = jnp.mean(stats[:, :local_groups], axis=0)
    mean_offsets = stats[:, :local_groups] - group_mean[None]
    group_var = (
        jnp.sum(stats[:, local_groups:], axis=0)
        + block_count * jnp.sum(mean_offsets * mean_offsets, axis=0)
    ) / (block_count * n_blocks)

    normed = (
        (grouped - group_mean[None, :, None]) * lax.rsqrt(group_var + 1e-06)[None, :, None]
    ).reshape(mixed.shape)
    activated = jax.nn.silu(normed * norm_gain + norm_bias)
    out_rows, out_cols, out_chan = (activated.shape[1], activated.shape[2], activated.shape[3])
    return activated.transpose(1, 2, 3, 0).reshape(out_rows, out_cols, out_chan * frames)


def solution(mesh):
    return jax.shard_map(
        per_device,
        mesh=mesh,
        in_specs=(
            P("sp", None, "section", "rep"),
            P(),
            P(),
            P(),
            P(),
            P(None, "sp", "section", None),
            P(),
            P(),
            P(None, None, None, "rep", None),
            P("rep"),
            P("rep"),
            P("rep"),
        ),
        out_specs=P("sp", "section", "rep"),
        check_vma=False,
    )
```

```python
import jax
import jax.numpy as jnp
from jax import lax
from jax.experimental import pallas as pl
from jax.experimental.pallas import tpu as pltpu
from jax.sharding import PartitionSpec as P

D = 3072
LC = 16
CO = 256
GROUPS = 32
ALL = ("section", "sp", "rep")
BLOCKS = ("section", "sp")


def causal_front(volume):
    return jnp.concatenate([volume[:1], volume[:1], volume], axis=0)


def valid_conv(front, kernel, kernel_spec, precision_mode):
    result = lax.conv_general_dilated(
        front[None],
        kernel,
        (1, 1, 1),
        "VALID",
        dimension_numbers=("NDHWC", kernel_spec, "NDHWC"),
        precision=precision_mode,
        preferred_element_type=jnp.float32,
    )
    return result[0]


def shard_kernel(rep_ref, tok_ref, weight_ref, scale_ref, latent_ref, copies_ref):
    out_ref = copies_ref.at[0]
    weight = weight_ref[...] * (1.0 + scale_ref[...])
    width = weight.shape[0]
    band_cols = tok_ref.shape[1]
    record = width + 2
    for frame in range(tok_ref.shape[0]):
        for row in range(tok_ref.shape[2]):
            x = tok_ref[frame, :, row, :]
            mean = jnp.mean(x, axis=1, keepdims=True)
            centred = x - mean
            m2 = jnp.sum(centred * centred, axis=1, keepdims=True)
            projected = lax.dot_general(
                centred,
                weight,
                (((1,), (1,)), ((), ())),
                precision=lax.Precision.HIGHEST,
                preferred_element_type=jnp.float32,
            )
            for col in range(band_cols):
                base = ((frame * tok_ref.shape[2] + row) * band_cols + col) * record
                out_ref[:, pl.ds(base, width)] = projected[col : col + 1, :]
                out_ref[:, pl.ds(base + width, 1)] = mean[col : col + 1, :]
                out_ref[:, pl.ds(base + width + 1, 1)] = m2[col : col + 1, :]
    lines, lat_rows, channels = latent_ref.shape
    offset = tok_ref.shape[0] * tok_ref.shape[2] * band_cols * record
    share = latent_ref[...]
    for line in range(lines):
        for row in range(lat_rows):
            out_ref[:, pl.ds(offset + (line * lat_rows + row) * channels, channels)] = share[
                line, row : row + 1, :
            ]
    row_value = out_ref[...]
    for copy in range(1, copies_ref.shape[0]):
        copies_ref[copy] = row_value


def shard_moments(tokens, proj_weight, mod_scale, latent_lines, share, rep, copies):
    tok_frames, patch_rows, band_cols, local_width = tokens.shape
    out_width = proj_weight.shape[0]
    size = tok_frames * patch_rows * band_cols * (out_width + 2) + latent_lines[0].size * share
    whole = lambda i, r: (0, 0, 0, 0)
    whole3 = lambda i, r: (0, 0, 0)
    return pl.pallas_call(
        shard_kernel,
        grid_spec=pltpu.PrefetchScalarGridSpec(
            num_scalar_prefetch=1,
            grid=(1,),
            in_specs=[
                pl.BlockSpec((tok_frames, band_cols, patch_rows, local_width), whole),
                pl.BlockSpec((out_width, local_width), lambda i, r: (0, r[0])),
                pl.BlockSpec((1, local_width), lambda i, r: (0, r[0])),
                pl.BlockSpec(
                    (share,) + latent_lines.shape[1:],
                    (lambda i, r: (r[0], 0, 0)) if share < latent_lines.shape[0] else whole3,
                ),
            ],
            out_specs=pl.BlockSpec((copies, 1, size), whole3),
        ),
        out_shape=jax.ShapeDtypeStruct((copies, 1, size), jnp.float32),
    )(
        rep.reshape(1).astype(jnp.int32),
        tokens.transpose(0, 2, 1, 3),
        proj_weight,
        mod_scale.reshape(1, -1),
        latent_lines,
    )


def neighbours(stack, index, axis):
    pad = [(0, 0)] * stack.ndim
    pad[axis] = (1, 1)
    return lax.dynamic_slice_in_dim(jnp.pad(stack, pad), index, 3, axis)


def per_device(
    tokens,
    mod_scale,
    mod_shift,
    proj_weight,
    proj_bias,
    noisy_latent,
    in_weight,
    in_bias,
    conv_weight,
    conv_bias,
    norm_gain,
    norm_bias,
):
    n_sec, n_sp, n_rep = (lax.axis_size(a) for a in ALL)
    n_dev = n_sec * n_sp * n_rep
    sec, spi, rep = (lax.axis_index(a) for a in ALL)
    tok_frames, patch_rows, band_cols, local_width = tokens.shape
    frames, lat_rows, lat_cols, _ = noisy_latent.shape
    full_width = local_width * n_rep
    out_width = proj_weight.shape[0]


    lines = frames * lat_cols
    stored = noisy_latent.transpose(0, 2, 1, 3).reshape(lines, lat_rows, LC)
    share = lines // n_rep if lines % n_rep == 0 else lines
    slab = lat_rows // 2
    every_row = patch_rows <= slab + 2
    payload = shard_moments(
        tokens, proj_weight, mod_scale, stored, share, rep, n_dev if every_row else 1
    )
    part_flat = tok_frames * patch_rows * band_cols * (out_width + 2)

    if every_row:
        window = patch_rows
        part_size = part_flat
        send = payload
    else:
        payload = payload[0, 0]
        window = slab + 2
        partial = payload[:part_flat].reshape(tok_frames, patch_rows, band_cols, out_width + 2)
        padded = jnp.pad(partial, ((0, 0), (1, 1), (0, 0), (0, 0)))
        per_slab = jnp.stack([padded[:, p * slab : p * slab + window] for p in range(n_sp)])
        per_slab = per_slab.reshape(n_sp, -1)
        part_size = per_slab.shape[1]
        latent_part = payload[part_flat:]
        send = jnp.concatenate(
            [
                jnp.broadcast_to(per_slab[None, :, None], (n_sec, n_sp, n_rep, part_size)),
                jnp.broadcast_to(latent_part, (n_sec, n_sp, n_rep, latent_part.shape[0])),
            ],
            axis=-1,
        ).reshape(n_dev, -1)
    received = lax.all_to_all(send, ALL, 0, 0, tiled=False).reshape(n_sec, n_sp, n_rep, -1)

    scaled_weight = proj_weight * (1.0 + mod_scale)[None, :]
    shard_columns = jnp.sum(scaled_weight.reshape(out_width, n_rep, local_width), axis=2).T
    shift_column = (
        jnp.dot(
            proj_weight,
            mod_shift,
            precision=lax.Precision.HIGHEST,
            preferred_element_type=jnp.float32,
        )
        + proj_bias
    )
    parts = neighbours(received[..., :part_size], sec, 0).reshape(
        3, n_sp, n_rep, tok_frames, window, band_cols, out_width + 2
    )
    means = parts[..., out_width]
    mean = jnp.mean(means, axis=2)
    offsets = means - mean[:, :, None]
    m2 = jnp.sum(parts[..., out_width + 1], axis=2) + local_width * jnp.sum(
        offsets * offsets, axis=2
    )
    token_var = m2 / full_width
    centred_proj = jnp.sum(parts[..., :out_width], axis=2) + lax.dot_general(
        offsets,
        shard_columns,
        (((2,), (0,)), ((), ())),
        precision=lax.Precision.HIGHEST,
        preferred_element_type=jnp.float32,
    )
    velocity = lax.rsqrt(token_var + 1e-06)[..., None] * centred_proj + shift_column
    patches = (
        velocity.reshape(3, frames, window, band_cols, LC, 2, 2)
        .transpose(1, 2, 5, 0, 3, 6, 4)
        .reshape(frames, 2 * window, 3 * 2 * band_cols, LC)
    )

    shares = neighbours(received[..., part_size:], sec, 0)
    if share == lines:
        shares = shares[:, :, 0]
    latent = shares.reshape(3, n_sp, frames, lat_cols, lat_rows, LC).transpose(0, 1, 2, 4, 3, 5)
    if window == patch_rows:
        latent = latent.transpose(2, 1, 3, 0, 4, 5).reshape(
            frames, n_sp * lat_rows, 3 * lat_cols, LC
        )
        clean = latent - 0.5 * patches
        clean = jnp.pad(clean, ((0, 0), (2, 2), (0, 0), (0, 0)))
        clean = lax.dynamic_slice_in_dim(clean, spi * lat_rows, lat_rows + 4, 1)
    else:
        latent = neighbours(latent.transpose(1, 2, 3, 0, 4, 5), spi, 0)
        latent = latent.transpose(1, 0, 2, 3, 4, 5).reshape(
            frames, 3 * lat_rows, 3 * lat_cols, LC
        )[:, lat_rows - 2 : 2 * lat_rows + 2]
        clean = latent - 0.5 * patches
    clean = clean[:, :, lat_cols - 2 : 2 * lat_cols + 2]

    row_global = spi * lat_rows - 2 + jnp.arange(lat_rows + 4)
    col_global = sec * lat_cols - 2 + jnp.arange(lat_cols + 4)
    row_inside = (row_global >= 0) & (row_global < lat_rows * n_sp)
    col_inside = (col_global >= 0) & (col_global < lat_cols * n_sec)
    clean = jnp.where(row_inside[None, :, None, None] & col_inside[None, None, :, None], clean, 0.0)

    inner_features = valid_conv(causal_front(clean), in_weight, "DHWIO", lax.Precision.HIGH) + in_bias
    inside = row_inside[None, 1:-1, None, None] & col_inside[None, None, 1:-1, None]
    features = causal_front(jnp.where(inside, inner_features, 0.0).astype(jnp.bfloat16))
    upsampled = jnp.repeat(jnp.repeat(features, 2, axis=1), 2, axis=2)[:, 1:-1, 1:-1, :]
    mixed = valid_conv(upsampled, conv_weight, "DHWOI", None) + conv_bias

    group_size = CO // GROUPS
    local_groups = mixed.shape[-1] // group_size
    grouped = mixed.reshape(-1, local_groups, group_size)
    block_count = grouped.shape[0] * group_size
    block_mean = jnp.sum(grouped, axis=(0, 2)) / block_count
    deviation = grouped - block_mean[None, :, None]
    block_m2 = jnp.sum(deviation * deviation, axis=(0, 2))
    n_blocks = n_sec * n_sp
    stats = jnp.broadcast_to(
        jnp.concatenate([block_mean, block_m2])[None], (n_blocks, 2 * local_groups)
    )
    stats = lax.all_to_all(stats, BLOCKS, 0, 0, tiled=False)
    group_mean = jnp.mean(stats[:, :local_groups], axis=0)
    mean_offsets = stats[:, :local_groups] - group_mean[None]
    group_var = (
        jnp.sum(stats[:, local_groups:], axis=0)
        + block_count * jnp.sum(mean_offsets * mean_offsets, axis=0)
    ) / (block_count * n_blocks)

    normed = (
        (grouped - group_mean[None, :, None]) * lax.rsqrt(group_var + 1e-06)[None, :, None]
    ).reshape(mixed.shape)
    activated = jax.nn.silu(normed * norm_gain + norm_bias)
    out_rows, out_cols, out_chan = (activated.shape[1], activated.shape[2], activated.shape[3])
    return activated.transpose(1, 2, 3, 0).reshape(out_rows, out_cols, out_chan * frames)


def solution(mesh):
    return jax.shard_map(
        per_device,
        mesh=mesh,
        in_specs=(
            P("sp", None, "section", "rep"),
            P(),
            P(),
            P(),
            P(),
            P(None, "sp", "section", None),
            P(),
            P(),
            P(None, None, None, "rep", None),
            P("rep"),
            P("rep"),
            P("rep"),
        ),
        out_specs=P("sp", "section", "rep"),
        check_vma=False,
    )
```

```python
import jax
import jax.numpy as jnp
from jax import lax
from jax.experimental import pallas as pl
from jax.experimental.pallas import tpu as pltpu
from jax.sharding import PartitionSpec as P

D = 3072
LC = 16
CO = 256
GROUPS = 32
ALL = ("section", "sp", "rep")
BLOCKS = ("section", "sp")


def causal_front(volume):
    return jnp.concatenate([volume[:1], volume[:1], volume], axis=0)


def valid_conv(front, kernel, kernel_spec, precision_mode):
    result = lax.conv_general_dilated(
        front[None],
        kernel,
        (1, 1, 1),
        "VALID",
        dimension_numbers=("NDHWC", kernel_spec, "NDHWC"),
        precision=precision_mode,
        preferred_element_type=jnp.float32,
    )
    return result[0]


def shard_kernel(rep_ref, tok_ref, weight_ref, scale_ref, latent_ref, copies_ref):
    out_ref = copies_ref.at[0]
    weight = weight_ref[...] * (1.0 + scale_ref[...])
    width = weight.shape[0]
    band_cols = tok_ref.shape[1]
    record = width + 2
    for frame in range(tok_ref.shape[0]):
        for row in range(tok_ref.shape[2]):
            x = tok_ref[frame, :, row, :]
            mean = jnp.mean(x, axis=1, keepdims=True)
            centred = x - mean
            m2 = jnp.sum(centred * centred, axis=1, keepdims=True)
            projected = lax.dot_general(
                centred,
                weight,
                (((1,), (1,)), ((), ())),
                precision=lax.Precision.HIGHEST,
                preferred_element_type=jnp.float32,
            )
            for col in range(band_cols):
                base = ((frame * tok_ref.shape[2] + row) * band_cols + col) * record
                out_ref[:, pl.ds(base, width)] = projected[col : col + 1, :]
                out_ref[:, pl.ds(base + width, 1)] = mean[col : col + 1, :]
                out_ref[:, pl.ds(base + width + 1, 1)] = m2[col : col + 1, :]
    lines, lat_rows, channels = latent_ref.shape
    offset = tok_ref.shape[0] * tok_ref.shape[2] * band_cols * record
    share = latent_ref[...]
    for line in range(lines):
        for row in range(lat_rows):
            out_ref[:, pl.ds(offset + (line * lat_rows + row) * channels, channels)] = share[
                line, row : row + 1, :
            ]
    row_value = out_ref[...]
    for copy in range(1, copies_ref.shape[0]):
        copies_ref[copy] = row_value


def shard_moments(tokens, proj_weight, mod_scale, latent_lines, share, rep, copies):
    tok_frames, patch_rows, band_cols, local_width = tokens.shape
    out_width = proj_weight.shape[0]
    size = tok_frames * patch_rows * band_cols * (out_width + 2) + latent_lines[0].size * share
    whole = lambda i, r: (0, 0, 0, 0)
    whole3 = lambda i, r: (0, 0, 0)
    return pl.pallas_call(
        shard_kernel,
        grid_spec=pltpu.PrefetchScalarGridSpec(
            num_scalar_prefetch=1,
            grid=(1,),
            in_specs=[
                pl.BlockSpec((tok_frames, band_cols, patch_rows, local_width), whole),
                pl.BlockSpec((out_width, local_width), lambda i, r: (0, r[0])),
                pl.BlockSpec((1, local_width), lambda i, r: (0, r[0])),
                pl.BlockSpec(
                    (share,) + latent_lines.shape[1:],
                    (lambda i, r: (r[0], 0, 0)) if share < latent_lines.shape[0] else whole3,
                ),
            ],
            out_specs=pl.BlockSpec((copies, 1, size), whole3),
        ),
        out_shape=jax.ShapeDtypeStruct((copies, 1, size), jnp.float32),
    )(
        rep.reshape(1).astype(jnp.int32),
        tokens.transpose(0, 2, 1, 3),
        proj_weight,
        mod_scale.reshape(1, -1),
        latent_lines,
    )


def neighbours(stack, index, axis):
    pad = [(0, 0)] * stack.ndim
    pad[axis] = (1, 1)
    return lax.dynamic_slice_in_dim(jnp.pad(stack, pad), index, 3, axis)


def per_device(
    tokens,
    mod_scale,
    mod_shift,
    proj_weight,
    proj_bias,
    noisy_latent,
    in_weight,
    in_bias,
    conv_weight,
    conv_bias,
    norm_gain,
    norm_bias,
):
    n_sec, n_sp, n_rep = (lax.axis_size(a) for a in ALL)
    n_dev = n_sec * n_sp * n_rep
    sec, spi, rep = (lax.axis_index(a) for a in ALL)
    tok_frames, patch_rows, band_cols, local_width = tokens.shape
    frames, lat_rows, lat_cols, _ = noisy_latent.shape
    full_width = local_width * n_rep
    out_width = proj_weight.shape[0]


    lines = frames * lat_cols
    stored = noisy_latent.transpose(0, 2, 1, 3).reshape(lines, lat_rows, LC)
    share = lines // n_rep if lines % n_rep == 0 else lines
    slab = lat_rows // 2
    every_row = patch_rows <= slab + 2
    payload = shard_moments(
        tokens, proj_weight, mod_scale, stored, share, rep, n_dev if every_row else 1
    )
    part_flat = tok_frames * patch_rows * band_cols * (out_width + 2)

    if every_row:
        window = patch_rows
        part_size = part_flat
        send = payload
    else:
        payload = payload[0, 0]
        window = slab + 2
        partial = payload[:part_flat].reshape(tok_frames, patch_rows, band_cols, out_width + 2)
        padded = jnp.pad(partial, ((0, 0), (1, 1), (0, 0), (0, 0)))
        per_slab = jnp.stack([padded[:, p * slab : p * slab + window] for p in range(n_sp)])
        per_slab = per_slab.reshape(n_sp, -1)
        part_size = per_slab.shape[1]
        latent_part = payload[part_flat:]
        send = jnp.concatenate(
            [
                jnp.broadcast_to(per_slab[None, :, None], (n_sec, n_sp, n_rep, part_size)),
                jnp.broadcast_to(latent_part, (n_sec, n_sp, n_rep, latent_part.shape[0])),
            ],
            axis=-1,
        ).reshape(n_dev, -1)
    received = lax.all_to_all(send, ALL, 0, 0, tiled=False).reshape(n_sec, n_sp, n_rep, -1)

    scaled_weight = proj_weight * (1.0 + mod_scale)[None, :]
    shard_columns = jnp.sum(scaled_weight.reshape(out_width, n_rep, local_width), axis=2).T
    shift_column = (
        jnp.dot(
            proj_weight,
            mod_shift,
            precision=lax.Precision.HIGHEST,
            preferred_element_type=jnp.float32,
        )
        + proj_bias
    )
    parts = neighbours(received[..., :part_size], sec, 0).reshape(
        3, n_sp, n_rep, tok_frames, window, band_cols, out_width + 2
    )
    means = parts[..., out_width]
    mean = jnp.mean(means, axis=2)
    offsets = means - mean[:, :, None]
    m2 = jnp.sum(parts[..., out_width + 1], axis=2) + local_width * jnp.sum(
        offsets * offsets, axis=2
    )
    token_var = m2 / full_width
    centred_proj = jnp.sum(parts[..., :out_width], axis=2) + lax.dot_general(
        offsets,
        shard_columns,
        (((2,), (0,)), ((), ())),
        precision=lax.Precision.HIGHEST,
        preferred_element_type=jnp.float32,
    )
    velocity = lax.rsqrt(token_var + 1e-06)[..., None] * centred_proj + shift_column
    patches = (
        velocity.reshape(3, frames, window, band_cols, LC, 2, 2)
        .transpose(1, 2, 5, 0, 3, 6, 4)
        .reshape(frames, 2 * window, 3 * 2 * band_cols, LC)
    )

    shares = neighbours(received[..., part_size:], sec, 0)
    if share == lines:
        shares = shares[:, :, 0]
    latent = shares.reshape(3, n_sp, frames, lat_cols, lat_rows, LC).transpose(0, 1, 2, 4, 3, 5)
    if window == patch_rows:
        latent = latent.transpose(2, 1, 3, 0, 4, 5).reshape(
            frames, n_sp * lat_rows, 3 * lat_cols, LC
        )
        clean = latent - 0.5 * patches
        clean = jnp.pad(clean, ((0, 0), (2, 2), (0, 0), (0, 0)))
        clean = lax.dynamic_slice_in_dim(clean, spi * lat_rows, lat_rows + 4, 1)
    else:
        latent = neighbours(latent.transpose(1, 2, 3, 0, 4, 5), spi, 0)
        latent = latent.transpose(1, 0, 2, 3, 4, 5).reshape(
            frames, 3 * lat_rows, 3 * lat_cols, LC
        )[:, lat_rows - 2 : 2 * lat_rows + 2]
        clean = latent - 0.5 * patches
    clean = clean[:, :, lat_cols - 2 : 2 * lat_cols + 2]

    row_global = spi * lat_rows - 2 + jnp.arange(lat_rows + 4)
    col_global = sec * lat_cols - 2 + jnp.arange(lat_cols + 4)
    row_inside = (row_global >= 0) & (row_global < lat_rows * n_sp)
    col_inside = (col_global >= 0) & (col_global < lat_cols * n_sec)
    clean = jnp.where(row_inside[None, :, None, None] & col_inside[None, None, :, None], clean, 0.0)

    inner_features = valid_conv(causal_front(clean), in_weight, "DHWIO", lax.Precision.HIGH) + in_bias
    inside = row_inside[None, 1:-1, None, None] & col_inside[None, None, 1:-1, None]
    features = causal_front(jnp.where(inside, inner_features, 0.0).astype(jnp.bfloat16))
    upsampled = jnp.repeat(jnp.repeat(features, 2, axis=1), 2, axis=2)[:, 1:-1, 1:-1, :]
    mixed = valid_conv(upsampled, conv_weight, "DHWOI", None) + conv_bias

    group_size = CO // GROUPS
    local_chan = mixed.shape[-1]
    local_groups = local_chan // group_size
    flat = mixed.reshape(-1, local_chan)
    cell_count = flat.shape[0]
    chan_mean = jnp.sum(flat, axis=0) / cell_count
    deviation = flat - chan_mean[None, :]
    chan_m2 = jnp.sum(deviation * deviation, axis=0)
    n_blocks = n_sec * n_sp
    stats = jnp.broadcast_to(
        jnp.concatenate([chan_mean, chan_m2])[None], (n_blocks, 2 * local_chan)
    )
    stats = lax.all_to_all(stats, BLOCKS, 0, 0, tiled=False)
    means = stats[:, :local_chan].reshape(n_blocks, local_groups, group_size)
    m2s = stats[:, local_chan:].reshape(n_blocks, local_groups, group_size)
    group_mean = jnp.mean(means, axis=(0, 2))
    mean_offsets = means - group_mean[None, :, None]
    group_var = (
        jnp.sum(m2s, axis=(0, 2)) + cell_count * jnp.sum(mean_offsets * mean_offsets, axis=(0, 2))
    ) / (cell_count * n_blocks * group_size)
    grouped = mixed.reshape(-1, local_groups, group_size)

    normed = (
        (grouped - group_mean[None, :, None]) * lax.rsqrt(group_var + 1e-06)[None, :, None]
    ).reshape(mixed.shape)
    activated = jax.nn.silu(normed * norm_gain + norm_bias)
    out_rows, out_cols, out_chan = (activated.shape[1], activated.shape[2], activated.shape[3])
    return activated.transpose(1, 2, 3, 0).reshape(out_rows, out_cols, out_chan * frames)


def solution(mesh):
    return jax.shard_map(
        per_device,
        mesh=mesh,
        in_specs=(
            P("sp", None, "section", "rep"),
            P(),
            P(),
            P(),
            P(),
            P(None, "sp", "section", None),
            P(),
            P(),
            P(None, None, None, "rep", None),
            P("rep"),
            P("rep"),
            P("rep"),
        ),
        out_specs=P("sp", "section", "rep"),
        check_vma=False,
    )
```

```python
import jax
import jax.numpy as jnp
from jax import lax
from jax.experimental import pallas as pl
from jax.experimental.pallas import tpu as pltpu
from jax.sharding import PartitionSpec as P

D = 3072
LC = 16
CO = 256
GROUPS = 32
ALL = ("section", "sp", "rep")
BLOCKS = ("section", "sp")


def causal_front(volume):
    return jnp.concatenate([volume[:1], volume[:1], volume], axis=0)


def valid_conv(front, kernel, kernel_spec, precision_mode):
    result = lax.conv_general_dilated(
        front[None],
        kernel,
        (1, 1, 1),
        "VALID",
        dimension_numbers=("NDHWC", kernel_spec, "NDHWC"),
        precision=precision_mode,
        preferred_element_type=jnp.float32,
    )
    return result[0]


def shard_kernel(rep_ref, tok_ref, weight_ref, scale_ref, latent_ref, copies_ref):
    out_ref = copies_ref.at[0]
    weight = weight_ref[...] * (1.0 + scale_ref[...])
    width = weight.shape[0]
    band_cols = tok_ref.shape[1]
    record = width + 2
    for frame in range(tok_ref.shape[0]):
        for row in range(tok_ref.shape[2]):
            x = tok_ref[frame, :, row, :]
            mean = jnp.mean(x, axis=1, keepdims=True)
            centred = x - mean
            m2 = jnp.sum(centred * centred, axis=1, keepdims=True)
            projected = lax.dot_general(
                centred,
                weight,
                (((1,), (1,)), ((), ())),
                precision=lax.Precision.HIGHEST,
                preferred_element_type=jnp.float32,
            )
            for col in range(band_cols):
                base = ((frame * tok_ref.shape[2] + row) * band_cols + col) * record
                out_ref[:, pl.ds(base, width)] = projected[col : col + 1, :]
                out_ref[:, pl.ds(base + width, 1)] = mean[col : col + 1, :]
                out_ref[:, pl.ds(base + width + 1, 1)] = m2[col : col + 1, :]
    lines, lat_rows, channels = latent_ref.shape
    offset = tok_ref.shape[0] * tok_ref.shape[2] * band_cols * record
    share = latent_ref[...]
    for line in range(lines):
        for row in range(lat_rows):
            out_ref[:, pl.ds(offset + (line * lat_rows + row) * channels, channels)] = share[
                line, row : row + 1, :
            ]
    row_value = out_ref[...]
    for copy in range(1, copies_ref.shape[0]):
        copies_ref[copy] = row_value


def shard_moments(tokens, proj_weight, mod_scale, latent_lines, share, rep, copies):
    tok_frames, patch_rows, band_cols, local_width = tokens.shape
    out_width = proj_weight.shape[0]
    size = tok_frames * patch_rows * band_cols * (out_width + 2) + latent_lines[0].size * share
    whole = lambda i, r: (0, 0, 0, 0)
    whole3 = lambda i, r: (0, 0, 0)
    return pl.pallas_call(
        shard_kernel,
        grid_spec=pltpu.PrefetchScalarGridSpec(
            num_scalar_prefetch=1,
            grid=(1,),
            in_specs=[
                pl.BlockSpec((tok_frames, band_cols, patch_rows, local_width), whole),
                pl.BlockSpec((out_width, local_width), lambda i, r: (0, r[0])),
                pl.BlockSpec((1, local_width), lambda i, r: (0, r[0])),
                pl.BlockSpec(
                    (share,) + latent_lines.shape[1:],
                    (lambda i, r: (r[0], 0, 0)) if share < latent_lines.shape[0] else whole3,
                ),
            ],
            out_specs=pl.BlockSpec((copies, 1, size), whole3),
        ),
        out_shape=jax.ShapeDtypeStruct((copies, 1, size), jnp.float32),
    )(
        rep.reshape(1).astype(jnp.int32),
        tokens.transpose(0, 2, 1, 3),
        proj_weight,
        mod_scale.reshape(1, -1),
        latent_lines,
    )


def neighbours(stack, index, axis):
    pad = [(0, 0)] * stack.ndim
    pad[axis] = (1, 1)
    return lax.dynamic_slice_in_dim(jnp.pad(stack, pad), index, 3, axis)


def per_device(
    tokens,
    mod_scale,
    mod_shift,
    proj_weight,
    proj_bias,
    noisy_latent,
    in_weight,
    in_bias,
    conv_weight,
    conv_bias,
    norm_gain,
    norm_bias,
):
    n_sec, n_sp, n_rep = (lax.axis_size(a) for a in ALL)
    n_dev = n_sec * n_sp * n_rep
    sec, spi, rep = (lax.axis_index(a) for a in ALL)
    tok_frames, patch_rows, band_cols, local_width = tokens.shape
    frames, lat_rows, lat_cols, _ = noisy_latent.shape
    full_width = local_width * n_rep
    out_width = proj_weight.shape[0]


    lines = frames * lat_cols
    stored = noisy_latent.transpose(0, 2, 1, 3).reshape(lines, lat_rows, LC)
    share = lines // n_rep if lines % n_rep == 0 else lines
    slab = lat_rows // 2
    every_row = patch_rows <= slab + 2
    payload = shard_moments(
        tokens, proj_weight, mod_scale, stored, share, rep, n_dev if every_row else 1
    )
    part_flat = tok_frames * patch_rows * band_cols * (out_width + 2)

    if every_row:
        window = patch_rows
        part_size = part_flat
        send = payload
    else:
        payload = payload[0, 0]
        window = slab + 2
        partial = payload[:part_flat].reshape(tok_frames, patch_rows, band_cols, out_width + 2)
        padded = jnp.pad(partial, ((0, 0), (1, 1), (0, 0), (0, 0)))
        per_slab = jnp.stack([padded[:, p * slab : p * slab + window] for p in range(n_sp)])
        per_slab = per_slab.reshape(n_sp, -1)
        part_size = per_slab.shape[1]
        latent_part = payload[part_flat:]
        send = jnp.concatenate(
            [
                jnp.broadcast_to(per_slab[None, :, None], (n_sec, n_sp, n_rep, part_size)),
                jnp.broadcast_to(latent_part, (n_sec, n_sp, n_rep, latent_part.shape[0])),
            ],
            axis=-1,
        ).reshape(n_dev, -1)
    received = lax.all_to_all(send, ALL, 0, 0, tiled=False).reshape(n_sec, n_sp, n_rep, -1)

    shard_of = jnp.arange(full_width) // local_width
    selector = jnp.concatenate(
        [
            jnp.where(
                shard_of[:, None] == jnp.arange(n_rep)[None, :], (1.0 + mod_scale)[:, None], 0.0
            ),
            mod_shift[:, None],
        ],
        axis=1,
    )
    folded = jnp.dot(
        proj_weight,
        selector,
        precision=lax.Precision.HIGHEST,
        preferred_element_type=jnp.float32,
    )
    shard_columns = folded[:, :n_rep].T
    shift_column = folded[:, n_rep] + proj_bias
    parts = neighbours(received[..., :part_size], sec, 0).reshape(
        3, n_sp, n_rep, tok_frames, window, band_cols, out_width + 2
    )
    means = parts[..., out_width]
    mean = jnp.mean(means, axis=2)
    offsets = means - mean[:, :, None]
    m2 = jnp.sum(parts[..., out_width + 1], axis=2) + local_width * jnp.sum(
        offsets * offsets, axis=2
    )
    token_var = m2 / full_width
    centred_proj = jnp.sum(parts[..., :out_width], axis=2) + lax.dot_general(
        offsets,
        shard_columns,
        (((2,), (0,)), ((), ())),
        precision=lax.Precision.HIGHEST,
        preferred_element_type=jnp.float32,
    )
    velocity = lax.rsqrt(token_var + 1e-06)[..., None] * centred_proj + shift_column
    patches = (
        velocity.reshape(3, frames, window, band_cols, LC, 2, 2)
        .transpose(1, 2, 5, 0, 3, 6, 4)
        .reshape(frames, 2 * window, 3 * 2 * band_cols, LC)
    )

    shares = neighbours(received[..., part_size:], sec, 0)
    if share == lines:
        shares = shares[:, :, 0]
    latent = shares.reshape(3, n_sp, frames, lat_cols, lat_rows, LC).transpose(0, 1, 2, 4, 3, 5)
    if window == patch_rows:
        latent = latent.transpose(2, 1, 3, 0, 4, 5).reshape(
            frames, n_sp * lat_rows, 3 * lat_cols, LC
        )
        clean = latent - 0.5 * patches
        clean = jnp.pad(clean, ((0, 0), (2, 2), (0, 0), (0, 0)))
        clean = lax.dynamic_slice_in_dim(clean, spi * lat_rows, lat_rows + 4, 1)
    else:
        latent = neighbours(latent.transpose(1, 2, 3, 0, 4, 5), spi, 0)
        latent = latent.transpose(1, 0, 2, 3, 4, 5).reshape(
            frames, 3 * lat_rows, 3 * lat_cols, LC
        )[:, lat_rows - 2 : 2 * lat_rows + 2]
        clean = latent - 0.5 * patches
    clean = clean[:, :, lat_cols - 2 : 2 * lat_cols + 2]

    row_global = spi * lat_rows - 2 + jnp.arange(lat_rows + 4)
    col_global = sec * lat_cols - 2 + jnp.arange(lat_cols + 4)
    row_inside = (row_global >= 0) & (row_global < lat_rows * n_sp)
    col_inside = (col_global >= 0) & (col_global < lat_cols * n_sec)
    clean = jnp.where(row_inside[None, :, None, None] & col_inside[None, None, :, None], clean, 0.0)

    inner_features = valid_conv(causal_front(clean), in_weight, "DHWIO", lax.Precision.HIGH) + in_bias
    inside = row_inside[None, 1:-1, None, None] & col_inside[None, None, 1:-1, None]
    features = causal_front(jnp.where(inside, inner_features, 0.0).astype(jnp.bfloat16))
    upsampled = jnp.repeat(jnp.repeat(features, 2, axis=1), 2, axis=2)[:, 1:-1, 1:-1, :]
    mixed = valid_conv(upsampled, conv_weight, "DHWOI", None) + conv_bias

    group_size = CO // GROUPS
    local_chan = mixed.shape[-1]
    local_groups = local_chan // group_size
    flat = mixed.reshape(-1, local_chan)
    cell_count = flat.shape[0]
    chan_mean = jnp.sum(flat, axis=0) / cell_count
    deviation = flat - chan_mean[None, :]
    chan_m2 = jnp.sum(deviation * deviation, axis=0)
    n_blocks = n_sec * n_sp
    stats = jnp.broadcast_to(
        jnp.concatenate([chan_mean, chan_m2])[None], (n_blocks, 2 * local_chan)
    )
    stats = lax.all_to_all(stats, BLOCKS, 0, 0, tiled=False)
    means = stats[:, :local_chan].reshape(n_blocks, local_groups, group_size)
    m2s = stats[:, local_chan:].reshape(n_blocks, local_groups, group_size)
    group_mean = jnp.mean(means, axis=(0, 2))
    mean_offsets = means - group_mean[None, :, None]
    group_var = (
        jnp.sum(m2s, axis=(0, 2)) + cell_count * jnp.sum(mean_offsets * mean_offsets, axis=(0, 2))
    ) / (cell_count * n_blocks * group_size)
    grouped = mixed.reshape(-1, local_groups, group_size)

    normed = (
        (grouped - group_mean[None, :, None]) * lax.rsqrt(group_var + 1e-06)[None, :, None]
    ).reshape(mixed.shape)
    activated = jax.nn.silu(normed * norm_gain + norm_bias)
    out_rows, out_cols, out_chan = (activated.shape[1], activated.shape[2], activated.shape[3])
    return activated.transpose(1, 2, 3, 0).reshape(out_rows, out_cols, out_chan * frames)


def solution(mesh):
    return jax.shard_map(
        per_device,
        mesh=mesh,
        in_specs=(
            P("sp", None, "section", "rep"),
            P(),
            P(),
            P(),
            P(),
            P(None, "sp", "section", None),
            P(),
            P(),
            P(None, None, None, "rep", None),
            P("rep"),
            P("rep"),
            P("rep"),
        ),
        out_specs=P("sp", "section", "rep"),
        check_vma=False,
    )
```

```python
import jax
import jax.numpy as jnp
from jax import lax
from jax.experimental import pallas as pl
from jax.experimental.pallas import tpu as pltpu
from jax.sharding import PartitionSpec as P

D = 3072
LC = 16
CO = 256
GROUPS = 32
ALL = ("section", "sp", "rep")
BLOCKS = ("section", "sp")


def causal_front(volume):
    return jnp.concatenate([volume[:1], volume[:1], volume], axis=0)


def valid_conv(front, kernel, kernel_spec, precision_mode):
    result = lax.conv_general_dilated(
        front[None],
        kernel,
        (1, 1, 1),
        "VALID",
        dimension_numbers=("NDHWC", kernel_spec, "NDHWC"),
        precision=precision_mode,
        preferred_element_type=jnp.float32,
    )
    return result[0]


def shard_kernel(rep_ref, tok_ref, weight_ref, scale_ref, latent_ref, copies_ref):
    out_ref = copies_ref.at[0]
    weight = weight_ref[...] * (1.0 + scale_ref[...])
    width = weight.shape[0]
    band_cols = tok_ref.shape[1]
    record = width + 2
    for frame in range(tok_ref.shape[0]):
        for row in range(tok_ref.shape[2]):
            x = tok_ref[frame, :, row, :]
            mean = jnp.mean(x, axis=1, keepdims=True)
            centred = x - mean
            m2 = jnp.sum(centred * centred, axis=1, keepdims=True)
            projected = lax.dot_general(
                centred,
                weight,
                (((1,), (1,)), ((), ())),
                precision=lax.Precision.HIGHEST,
                preferred_element_type=jnp.float32,
            )
            for col in range(band_cols):
                base = ((frame * tok_ref.shape[2] + row) * band_cols + col) * record
                out_ref[:, pl.ds(base, width)] = projected[col : col + 1, :]
                out_ref[:, pl.ds(base + width, 1)] = mean[col : col + 1, :]
                out_ref[:, pl.ds(base + width + 1, 1)] = m2[col : col + 1, :]
    lines, lat_rows, channels = latent_ref.shape
    offset = tok_ref.shape[0] * tok_ref.shape[2] * band_cols * record
    share = latent_ref[...]
    for line in range(lines):
        for row in range(lat_rows):
            out_ref[:, pl.ds(offset + (line * lat_rows + row) * channels, channels)] = share[
                line, row : row + 1, :
            ]
    row_value = out_ref[...]
    for copy in range(1, copies_ref.shape[0]):
        copies_ref[copy] = row_value


def shard_moments(tokens, proj_weight, mod_scale, latent_lines, share, rep, copies):
    tok_frames, patch_rows, band_cols, local_width = tokens.shape
    out_width = proj_weight.shape[0]
    size = tok_frames * patch_rows * band_cols * (out_width + 2) + latent_lines[0].size * share
    whole = lambda i, r: (0, 0, 0, 0)
    whole3 = lambda i, r: (0, 0, 0)
    return pl.pallas_call(
        shard_kernel,
        grid_spec=pltpu.PrefetchScalarGridSpec(
            num_scalar_prefetch=1,
            grid=(1,),
            in_specs=[
                pl.BlockSpec((tok_frames, band_cols, patch_rows, local_width), whole),
                pl.BlockSpec((out_width, local_width), lambda i, r: (0, r[0])),
                pl.BlockSpec((1, local_width), lambda i, r: (0, r[0])),
                pl.BlockSpec(
                    (share,) + latent_lines.shape[1:],
                    (lambda i, r: (r[0], 0, 0)) if share < latent_lines.shape[0] else whole3,
                ),
            ],
            out_specs=pl.BlockSpec((copies, 1, size), whole3),
        ),
        out_shape=jax.ShapeDtypeStruct((copies, 1, size), jnp.float32),
    )(
        rep.reshape(1).astype(jnp.int32),
        tokens.transpose(0, 2, 1, 3),
        proj_weight,
        mod_scale.reshape(1, -1),
        latent_lines,
    )


def neighbours(stack, index, axis):
    pad = [(0, 0)] * stack.ndim
    pad[axis] = (1, 1)
    return lax.dynamic_slice_in_dim(jnp.pad(stack, pad), index, 3, axis)


def per_device(
    tokens,
    mod_scale,
    mod_shift,
    proj_weight,
    proj_bias,
    noisy_latent,
    in_weight,
    in_bias,
    conv_weight,
    conv_bias,
    norm_gain,
    norm_bias,
):
    n_sec, n_sp, n_rep = (lax.axis_size(a) for a in ALL)
    n_dev = n_sec * n_sp * n_rep
    sec, spi, rep = (lax.axis_index(a) for a in ALL)
    tok_frames, patch_rows, band_cols, local_width = tokens.shape
    frames, lat_rows, lat_cols, _ = noisy_latent.shape
    full_width = local_width * n_rep
    out_width = proj_weight.shape[0]


    lines = frames * lat_cols
    stored = noisy_latent.transpose(0, 2, 1, 3).reshape(lines, lat_rows, LC)
    share = lines // n_rep if lines % n_rep == 0 else lines
    slab = lat_rows // 2
    every_row = patch_rows <= slab + 2
    payload = shard_moments(
        tokens, proj_weight, mod_scale, stored, share, rep, n_dev if every_row else 1
    )
    part_flat = tok_frames * patch_rows * band_cols * (out_width + 2)

    if every_row:
        window = patch_rows
        part_size = part_flat
        send = payload
    else:
        payload = payload[0, 0]
        window = slab + 2
        partial = payload[:part_flat].reshape(tok_frames, patch_rows, band_cols, out_width + 2)
        padded = jnp.pad(partial, ((0, 0), (1, 1), (0, 0), (0, 0)))
        per_slab = jnp.stack([padded[:, p * slab : p * slab + window] for p in range(n_sp)])
        per_slab = per_slab.reshape(n_sp, -1)
        part_size = per_slab.shape[1]
        latent_part = payload[part_flat:]
        send = jnp.concatenate(
            [
                jnp.broadcast_to(per_slab[None, :, None], (n_sec, n_sp, n_rep, part_size)),
                jnp.broadcast_to(latent_part, (n_sec, n_sp, n_rep, latent_part.shape[0])),
            ],
            axis=-1,
        ).reshape(n_dev, -1)
    received = lax.all_to_all(send, ALL, 0, 0, tiled=False).reshape(n_sec, n_sp, n_rep, -1)

    shard_of = jnp.arange(full_width) // local_width
    selector = jnp.concatenate(
        [
            jnp.where(
                shard_of[:, None] == jnp.arange(n_rep)[None, :], (1.0 + mod_scale)[:, None], 0.0
            ),
            mod_shift[:, None],
        ],
        axis=1,
    )
    folded = jnp.dot(
        proj_weight,
        selector,
        precision=lax.Precision.HIGHEST,
        preferred_element_type=jnp.float32,
    )
    shard_columns = folded[:, :n_rep].T
    shift_column = folded[:, n_rep] + proj_bias
    parts = neighbours(received[..., :part_size], sec, 0).reshape(
        3, n_sp, n_rep, tok_frames, window, band_cols, out_width + 2
    )
    means = parts[..., out_width]
    mean = jnp.mean(means, axis=2)
    offsets = means - mean[:, :, None]
    m2 = jnp.sum(parts[..., out_width + 1], axis=2) + local_width * jnp.sum(
        offsets * offsets, axis=2
    )
    token_var = m2 / full_width
    centred_proj = jnp.sum(parts[..., :out_width], axis=2) + lax.dot_general(
        offsets,
        shard_columns,
        (((2,), (0,)), ((), ())),
        precision=lax.Precision.HIGHEST,
        preferred_element_type=jnp.float32,
    )
    velocity = lax.rsqrt(token_var + 1e-06)[..., None] * centred_proj + shift_column
    patches = (
        velocity.reshape(3, frames, window, band_cols, LC, 2, 2)
        .transpose(1, 2, 5, 0, 3, 6, 4)
        .reshape(frames, 2 * window, 3 * 2 * band_cols, LC)
    )

    shares = neighbours(received[..., part_size:], sec, 0)
    if share == lines:
        shares = shares[:, :, 0]
    latent = shares.reshape(3, n_sp, frames, lat_cols, lat_rows, LC).transpose(0, 1, 2, 4, 3, 5)
    if window == patch_rows:
        latent = latent.transpose(2, 1, 3, 0, 4, 5).reshape(
            frames, n_sp * lat_rows, 3 * lat_cols, LC
        )
        clean = latent - 0.5 * patches
        clean = jnp.pad(clean, ((0, 0), (2, 2), (0, 0), (0, 0)))
        clean = lax.dynamic_slice_in_dim(clean, spi * lat_rows, lat_rows + 4, 1)
    else:
        latent = neighbours(latent.transpose(1, 2, 3, 0, 4, 5), spi, 0)
        latent = latent.transpose(1, 0, 2, 3, 4, 5).reshape(
            frames, 3 * lat_rows, 3 * lat_cols, LC
        )[:, lat_rows - 2 : 2 * lat_rows + 2]
        clean = latent - 0.5 * patches
    clean = clean[:, :, lat_cols - 2 : 2 * lat_cols + 2]

    row_global = spi * lat_rows - 2 + jnp.arange(lat_rows + 4)
    col_global = sec * lat_cols - 2 + jnp.arange(lat_cols + 4)
    row_inside = (row_global >= 0) & (row_global < lat_rows * n_sp)
    col_inside = (col_global >= 0) & (col_global < lat_cols * n_sec)
    clean = jnp.where(row_inside[None, :, None, None] & col_inside[None, None, :, None], clean, 0.0)

    inner_features = valid_conv(causal_front(clean), in_weight, "DHWIO", lax.Precision.HIGH) + in_bias
    inside = row_inside[None, 1:-1, None, None] & col_inside[None, None, 1:-1, None]
    features = causal_front(jnp.where(inside, inner_features, 0.0).astype(jnp.bfloat16))
    upsampled = jnp.repeat(jnp.repeat(features, 2, axis=1), 2, axis=2)[:, 1:-1, 1:-1, :]
    mixed = valid_conv(upsampled, conv_weight, "DHWOI", None) + conv_bias

    group_size = CO // GROUPS
    local_chan = mixed.shape[-1]
    local_groups = local_chan // group_size
    flat = mixed.reshape(-1, local_chan)
    cell_count = flat.shape[0]
    chan_mean = jnp.sum(flat, axis=0) / cell_count
    deviation = flat - chan_mean[None, :]
    chan_m2 = jnp.sum(deviation * deviation, axis=0)
    n_blocks = n_sec * n_sp
    stats = jnp.broadcast_to(
        jnp.concatenate([chan_mean, chan_m2])[None], (n_blocks, 2 * local_chan)
    )
    stats = lax.all_to_all(stats, BLOCKS, 0, 0, tiled=False)
    means = stats[:, :local_chan]
    group_mean = jnp.sum(means, axis=0).reshape(local_groups, group_size).sum(axis=1) / (
        n_blocks * group_size
    )
    chan_group_mean = jnp.repeat(group_mean, group_size)
    mean_offsets = means - chan_group_mean[None, :]
    chan_total = jnp.sum(stats[:, local_chan:], axis=0) + cell_count * jnp.sum(
        mean_offsets * mean_offsets, axis=0
    )
    group_var = chan_total.reshape(local_groups, group_size).sum(axis=1) / (
        cell_count * n_blocks * group_size
    )
    chan_scale = jnp.repeat(lax.rsqrt(group_var + 1e-06), group_size) * norm_gain
    activated = jax.nn.silu((mixed - chan_group_mean) * chan_scale + norm_bias)
    out_rows, out_cols, out_chan = (activated.shape[1], activated.shape[2], activated.shape[3])
    return activated.transpose(1, 2, 3, 0).reshape(out_rows, out_cols, out_chan * frames)


def solution(mesh):
    return jax.shard_map(
        per_device,
        mesh=mesh,
        in_specs=(
            P("sp", None, "section", "rep"),
            P(),
            P(),
            P(),
            P(),
            P(None, "sp", "section", None),
            P(),
            P(),
            P(None, None, None, "rep", None),
            P("rep"),
            P("rep"),
            P("rep"),
        ),
        out_specs=P("sp", "section", "rep"),
        check_vma=False,
    )
```

```python
import jax
import jax.numpy as jnp
from jax import lax
from jax.experimental import pallas as pl
from jax.experimental.pallas import tpu as pltpu
from jax.sharding import PartitionSpec as P

D = 3072
LC = 16
CO = 256
GROUPS = 32
ALL = ("section", "sp", "rep")
BLOCKS = ("section", "sp")


def causal_front(volume):
    return jnp.concatenate([volume[:1], volume[:1], volume], axis=0)


def valid_conv(front, kernel, kernel_spec, precision_mode):
    result = lax.conv_general_dilated(
        front[None],
        kernel,
        (1, 1, 1),
        "VALID",
        dimension_numbers=("NDHWC", kernel_spec, "NDHWC"),
        precision=precision_mode,
        preferred_element_type=jnp.float32,
    )
    return result[0]


def shard_kernel(rep_ref, tok_ref, weight_ref, scale_ref, latent_ref, copies_ref):
    out_ref = copies_ref.at[0]
    width = weight_ref.shape[0]
    new = lax.broadcasted_iota(jnp.int32, (width, width), 0)
    old = lax.broadcasted_iota(jnp.int32, (width, width), 1)
    quarter = width // 4
    order = jnp.where(old == 4 * (new % quarter) + new // quarter, 1.0, 0.0)
    weight = lax.dot_general(
        order,
        weight_ref[...] * (1.0 + scale_ref[...]),
        (((1,), (0,)), ((), ())),
        precision=lax.Precision.HIGHEST,
        preferred_element_type=jnp.float32,
    )
    band_cols = tok_ref.shape[1]
    record = width + 2
    for frame in range(tok_ref.shape[0]):
        for row in range(tok_ref.shape[2]):
            x = tok_ref[frame, :, row, :]
            mean = jnp.mean(x, axis=1, keepdims=True)
            centred = x - mean
            m2 = jnp.sum(centred * centred, axis=1, keepdims=True)
            projected = lax.dot_general(
                centred,
                weight,
                (((1,), (1,)), ((), ())),
                precision=lax.Precision.HIGHEST,
                preferred_element_type=jnp.float32,
            )
            for col in range(band_cols):
                base = ((frame * tok_ref.shape[2] + row) * band_cols + col) * record
                out_ref[:, pl.ds(base, width)] = projected[col : col + 1, :]
                out_ref[:, pl.ds(base + width, 1)] = mean[col : col + 1, :]
                out_ref[:, pl.ds(base + width + 1, 1)] = m2[col : col + 1, :]
    lines, lat_rows, channels = latent_ref.shape
    offset = tok_ref.shape[0] * tok_ref.shape[2] * band_cols * record
    share = latent_ref[...]
    for line in range(lines):
        for row in range(lat_rows):
            out_ref[:, pl.ds(offset + (line * lat_rows + row) * channels, channels)] = share[
                line, row : row + 1, :
            ]
    row_value = out_ref[...]
    for copy in range(1, copies_ref.shape[0]):
        copies_ref[copy] = row_value


def shard_moments(tokens, proj_weight, mod_scale, latent_lines, share, rep, copies):
    tok_frames, patch_rows, band_cols, local_width = tokens.shape
    out_width = proj_weight.shape[0]
    size = tok_frames * patch_rows * band_cols * (out_width + 2) + latent_lines[0].size * share
    whole = lambda i, r: (0, 0, 0, 0)
    whole3 = lambda i, r: (0, 0, 0)
    return pl.pallas_call(
        shard_kernel,
        grid_spec=pltpu.PrefetchScalarGridSpec(
            num_scalar_prefetch=1,
            grid=(1,),
            in_specs=[
                pl.BlockSpec((tok_frames, band_cols, patch_rows, local_width), whole),
                pl.BlockSpec((out_width, local_width), lambda i, r: (0, r[0])),
                pl.BlockSpec((1, local_width), lambda i, r: (0, r[0])),
                pl.BlockSpec(
                    (share,) + latent_lines.shape[1:],
                    (lambda i, r: (r[0], 0, 0)) if share < latent_lines.shape[0] else whole3,
                ),
            ],
            out_specs=pl.BlockSpec((copies, 1, size), whole3),
        ),
        out_shape=jax.ShapeDtypeStruct((copies, 1, size), jnp.float32),
    )(
        rep.reshape(1).astype(jnp.int32),
        tokens.transpose(0, 2, 1, 3),
        proj_weight,
        mod_scale.reshape(1, -1),
        latent_lines,
    )


def neighbours(stack, index, axis):
    pad = [(0, 0)] * stack.ndim
    pad[axis] = (1, 1)
    return lax.dynamic_slice_in_dim(jnp.pad(stack, pad), index, 3, axis)


def per_device(
    tokens,
    mod_scale,
    mod_shift,
    proj_weight,
    proj_bias,
    noisy_latent,
    in_weight,
    in_bias,
    conv_weight,
    conv_bias,
    norm_gain,
    norm_bias,
):
    n_sec, n_sp, n_rep = (lax.axis_size(a) for a in ALL)
    n_dev = n_sec * n_sp * n_rep
    sec, spi, rep = (lax.axis_index(a) for a in ALL)
    tok_frames, patch_rows, band_cols, local_width = tokens.shape
    frames, lat_rows, lat_cols, _ = noisy_latent.shape
    full_width = local_width * n_rep
    out_width = proj_weight.shape[0]


    lines = frames * lat_cols
    stored = noisy_latent.transpose(0, 2, 1, 3).reshape(lines, lat_rows, LC)
    share = lines // n_rep if lines % n_rep == 0 else lines
    slab = lat_rows // 2
    every_row = patch_rows <= slab + 2
    payload = shard_moments(
        tokens, proj_weight, mod_scale, stored, share, rep, n_dev if every_row else 1
    )
    part_flat = tok_frames * patch_rows * band_cols * (out_width + 2)

    if every_row:
        window = patch_rows
        part_size = part_flat
        send = payload
    else:
        payload = payload[0, 0]
        window = slab + 2
        partial = payload[:part_flat].reshape(tok_frames, patch_rows, band_cols, out_width + 2)
        padded = jnp.pad(partial, ((0, 0), (1, 1), (0, 0), (0, 0)))
        per_slab = jnp.stack([padded[:, p * slab : p * slab + window] for p in range(n_sp)])
        per_slab = per_slab.reshape(n_sp, -1)
        part_size = per_slab.shape[1]
        latent_part = payload[part_flat:]
        send = jnp.concatenate(
            [
                jnp.broadcast_to(per_slab[None, :, None], (n_sec, n_sp, n_rep, part_size)),
                jnp.broadcast_to(latent_part, (n_sec, n_sp, n_rep, latent_part.shape[0])),
            ],
            axis=-1,
        ).reshape(n_dev, -1)
    received = lax.all_to_all(send, ALL, 0, 0, tiled=False).reshape(n_sec, n_sp, n_rep, -1)

    scaled_weight = proj_weight * (1.0 + mod_scale)[None, :]
    shard_columns = jnp.sum(scaled_weight.reshape(out_width, n_rep, local_width), axis=2).T
    shift_column = (
        jnp.dot(
            proj_weight,
            mod_shift,
            precision=lax.Precision.HIGHEST,
            preferred_element_type=jnp.float32,
        )
        + proj_bias
    )
    by_parity = lambda v: v.reshape(v.shape[:-1] + (LC, 4)).swapaxes(-1, -2).reshape(v.shape)
    shard_columns = by_parity(shard_columns)
    shift_column = by_parity(shift_column)
    parts = neighbours(received[..., :part_size], sec, 0).reshape(
        3, n_sp, n_rep, tok_frames, window, band_cols, out_width + 2
    )
    means = parts[..., out_width]
    mean = jnp.mean(means, axis=2)
    offsets = means - mean[:, :, None]
    m2 = jnp.sum(parts[..., out_width + 1], axis=2) + local_width * jnp.sum(
        offsets * offsets, axis=2
    )
    token_var = m2 / full_width
    centred_proj = jnp.sum(parts[..., :out_width], axis=2) + lax.dot_general(
        offsets,
        shard_columns,
        (((2,), (0,)), ((), ())),
        precision=lax.Precision.HIGHEST,
        preferred_element_type=jnp.float32,
    )
    velocity = lax.rsqrt(token_var + 1e-06)[..., None] * centred_proj + shift_column
    patches = (
        velocity.reshape(3, frames, window, band_cols, 2, 2, LC)
        .transpose(1, 2, 4, 0, 3, 5, 6)
        .reshape(frames, 2 * window, 3 * 2 * band_cols, LC)
    )

    shares = neighbours(received[..., part_size:], sec, 0)
    if share == lines:
        shares = shares[:, :, 0]
    latent = shares.reshape(3, n_sp, frames, lat_cols, lat_rows, LC).transpose(0, 1, 2, 4, 3, 5)
    if window == patch_rows:
        latent = latent.transpose(2, 1, 3, 0, 4, 5).reshape(
            frames, n_sp * lat_rows, 3 * lat_cols, LC
        )
        clean = latent - 0.5 * patches
        clean = jnp.pad(clean, ((0, 0), (2, 2), (0, 0), (0, 0)))
        clean = lax.dynamic_slice_in_dim(clean, spi * lat_rows, lat_rows + 4, 1)
    else:
        latent = neighbours(latent.transpose(1, 2, 3, 0, 4, 5), spi, 0)
        latent = latent.transpose(1, 0, 2, 3, 4, 5).reshape(
            frames, 3 * lat_rows, 3 * lat_cols, LC
        )[:, lat_rows - 2 : 2 * lat_rows + 2]
        clean = latent - 0.5 * patches
    clean = clean[:, :, lat_cols - 2 : 2 * lat_cols + 2]

    row_global = spi * lat_rows - 2 + jnp.arange(lat_rows + 4)
    col_global = sec * lat_cols - 2 + jnp.arange(lat_cols + 4)
    row_inside = (row_global >= 0) & (row_global < lat_rows * n_sp)
    col_inside = (col_global >= 0) & (col_global < lat_cols * n_sec)
    clean = jnp.where(row_inside[None, :, None, None] & col_inside[None, None, :, None], clean, 0.0)

    inner_features = valid_conv(causal_front(clean), in_weight, "DHWIO", lax.Precision.HIGH) + in_bias
    inside = row_inside[None, 1:-1, None, None] & col_inside[None, None, 1:-1, None]
    features = causal_front(jnp.where(inside, inner_features, 0.0).astype(jnp.bfloat16))
    upsampled = jnp.repeat(jnp.repeat(features, 2, axis=1), 2, axis=2)[:, 1:-1, 1:-1, :]
    mixed = valid_conv(upsampled, conv_weight, "DHWOI", None) + conv_bias

    group_size = CO // GROUPS
    local_groups = mixed.shape[-1] // group_size
    grouped = mixed.reshape(-1, local_groups, group_size)
    block_count = grouped.shape[0] * group_size
    block_mean = jnp.sum(grouped, axis=(0, 2)) / block_count
    deviation = grouped - block_mean[None, :, None]
    block_m2 = jnp.sum(deviation * deviation, axis=(0, 2))
    n_blocks = n_sec * n_sp
    stats = jnp.broadcast_to(
        jnp.concatenate([block_mean, block_m2])[None], (n_blocks, 2 * local_groups)
    )
    stats = lax.all_to_all(stats, BLOCKS, 0, 0, tiled=False)
    group_mean = jnp.mean(stats[:, :local_groups], axis=0)
    mean_offsets = stats[:, :local_groups] - group_mean[None]
    group_var = (
        jnp.sum(stats[:, local_groups:], axis=0)
        + block_count * jnp.sum(mean_offsets * mean_offsets, axis=0)
    ) / (block_count * n_blocks)

    normed = (
        (grouped - group_mean[None, :, None]) * lax.rsqrt(group_var + 1e-06)[None, :, None]
    ).reshape(mixed.shape)
    activated = jax.nn.silu(normed * norm_gain + norm_bias)
    out_rows, out_cols, out_chan = (activated.shape[1], activated.shape[2], activated.shape[3])
    return activated.transpose(1, 2, 3, 0).reshape(out_rows, out_cols, out_chan * frames)


def solution(mesh):
    return jax.shard_map(
        per_device,
        mesh=mesh,
        in_specs=(
            P("sp", None, "section", "rep"),
            P(),
            P(),
            P(),
            P(),
            P(None, "sp", "section", None),
            P(),
            P(),
            P(None, None, None, "rep", None),
            P("rep"),
            P("rep"),
            P("rep"),
        ),
        out_specs=P("sp", "section", "rep"),
        check_vma=False,
    )
```

```python
import jax
import jax.numpy as jnp
from jax import lax
from jax.experimental import pallas as pl
from jax.experimental.pallas import tpu as pltpu
from jax.sharding import PartitionSpec as P

D = 3072
LC = 16
CO = 256
GROUPS = 32
ALL = ("section", "sp", "rep")
BLOCKS = ("section", "sp")


def causal_front(volume):
    return jnp.concatenate([volume[:1], volume[:1], volume], axis=0)


def valid_conv(front, kernel, kernel_spec, precision_mode):
    result = lax.conv_general_dilated(
        front[None],
        kernel,
        (1, 1, 1),
        "VALID",
        dimension_numbers=("NDHWC", kernel_spec, "NDHWC"),
        precision=precision_mode,
        preferred_element_type=jnp.float32,
    )
    return result[0]


def shard_kernel(rep_ref, tok_ref, weight_ref, scale_ref, latent_ref, copies_ref):
    out_ref = copies_ref.at[0]
    weight = weight_ref[...] * (1.0 + scale_ref[...])
    width = weight.shape[0]
    band_cols = tok_ref.shape[1]
    record = width + 2
    for frame in range(tok_ref.shape[0]):
        for row in range(tok_ref.shape[2]):
            x = tok_ref[frame, :, row, :]
            mean = jnp.mean(x, axis=1, keepdims=True)
            centred = x - mean
            m2 = jnp.sum(centred * centred, axis=1, keepdims=True)
            projected = lax.dot_general(
                centred,
                weight,
                (((1,), (1,)), ((), ())),
                precision=lax.Precision.HIGHEST,
                preferred_element_type=jnp.float32,
            )
            for col in range(band_cols):
                base = ((frame * tok_ref.shape[2] + row) * band_cols + col) * record
                out_ref[:, pl.ds(base, width)] = projected[col : col + 1, :]
                out_ref[:, pl.ds(base + width, 1)] = mean[col : col + 1, :]
                out_ref[:, pl.ds(base + width + 1, 1)] = m2[col : col + 1, :]
    lines, lat_rows, channels = latent_ref.shape
    offset = tok_ref.shape[0] * tok_ref.shape[2] * band_cols * record
    share = latent_ref[...]
    for line in range(lines):
        for row in range(lat_rows):
            out_ref[:, pl.ds(offset + (line * lat_rows + row) * channels, channels)] = share[
                line, row : row + 1, :
            ]
    row_value = out_ref[...]
    for copy in range(1, copies_ref.shape[0]):
        copies_ref[copy] = row_value


def shard_moments(tokens, proj_weight, mod_scale, latent_lines, share, rep, copies):
    tok_frames, patch_rows, band_cols, local_width = tokens.shape
    out_width = proj_weight.shape[0]
    size = tok_frames * patch_rows * band_cols * (out_width + 2) + latent_lines[0].size * share
    whole = lambda i, r: (0, 0, 0, 0)
    whole3 = lambda i, r: (0, 0, 0)
    return pl.pallas_call(
        shard_kernel,
        grid_spec=pltpu.PrefetchScalarGridSpec(
            num_scalar_prefetch=1,
            grid=(1,),
            in_specs=[
                pl.BlockSpec((tok_frames, band_cols, patch_rows, local_width), whole),
                pl.BlockSpec((out_width, local_width), lambda i, r: (0, r[0])),
                pl.BlockSpec((1, local_width), lambda i, r: (0, r[0])),
                pl.BlockSpec(
                    (share,) + latent_lines.shape[1:],
                    (lambda i, r: (r[0], 0, 0)) if share < latent_lines.shape[0] else whole3,
                ),
            ],
            out_specs=pl.BlockSpec((copies, 1, size), whole3),
        ),
        out_shape=jax.ShapeDtypeStruct((copies, 1, size), jnp.float32),
    )(
        rep.reshape(1).astype(jnp.int32),
        tokens.transpose(0, 2, 1, 3),
        proj_weight,
        mod_scale.reshape(1, -1),
        latent_lines,
    )


def neighbours(stack, index, axis):
    pad = [(0, 0)] * stack.ndim
    pad[axis] = (1, 1)
    return lax.dynamic_slice_in_dim(jnp.pad(stack, pad), index, 3, axis)


def per_device(
    tokens,
    mod_scale,
    mod_shift,
    proj_weight,
    proj_bias,
    noisy_latent,
    in_weight,
    in_bias,
    conv_weight,
    conv_bias,
    norm_gain,
    norm_bias,
):
    n_sec, n_sp, n_rep = (lax.axis_size(a) for a in ALL)
    n_dev = n_sec * n_sp * n_rep
    sec, spi, rep = (lax.axis_index(a) for a in ALL)
    tok_frames, patch_rows, band_cols, local_width = tokens.shape
    frames, lat_rows, lat_cols, _ = noisy_latent.shape
    full_width = local_width * n_rep
    out_width = proj_weight.shape[0]


    lines = frames * lat_cols
    stored = noisy_latent.transpose(0, 2, 1, 3).reshape(lines, lat_rows, LC)
    share = lines // n_rep if lines % n_rep == 0 else lines
    slab = lat_rows // 2
    every_row = patch_rows <= slab + 2
    payload = shard_moments(
        tokens, proj_weight, mod_scale, stored, share, rep, n_dev if every_row else 1
    )
    part_flat = tok_frames * patch_rows * band_cols * (out_width + 2)

    if every_row:
        window = patch_rows
        part_size = part_flat
        send = payload
    else:
        payload = payload[0, 0]
        window = slab + 2
        partial = payload[:part_flat].reshape(tok_frames, patch_rows, band_cols, out_width + 2)
        padded = jnp.pad(partial, ((0, 0), (1, 1), (0, 0), (0, 0)))
        per_slab = jnp.stack([padded[:, p * slab : p * slab + window] for p in range(n_sp)])
        per_slab = per_slab.reshape(n_sp, -1)
        part_size = per_slab.shape[1]
        latent_part = payload[part_flat:]
        send = jnp.concatenate(
            [
                jnp.broadcast_to(per_slab[None, :, None], (n_sec, n_sp, n_rep, part_size)),
                jnp.broadcast_to(latent_part, (n_sec, n_sp, n_rep, latent_part.shape[0])),
            ],
            axis=-1,
        ).reshape(n_dev, -1)
    received = lax.all_to_all(send, ALL, 0, 0, tiled=False).reshape(n_sec, n_sp, n_rep, -1)

    scaled_weight = proj_weight * (1.0 + mod_scale)[None, :]
    shard_columns = jnp.sum(scaled_weight.reshape(out_width, n_rep, local_width), axis=2).T
    shift_column = (
        jnp.dot(
            proj_weight,
            mod_shift,
            precision=lax.Precision.HIGHEST,
            preferred_element_type=jnp.float32,
        )
        + proj_bias
    )
    def halo_band(stack, width, axis):
        return jnp.concatenate(
            [
                lax.slice_in_dim(stack[0], stack.shape[axis] - width, None, axis=axis - 1),
                stack[1],
                lax.slice_in_dim(stack[2], 0, width, axis=axis - 1),
            ],
            axis=axis - 1,
        )

    parts = neighbours(received[..., :part_size], sec, 0).reshape(
        3, n_sp, n_rep, tok_frames, window, band_cols, out_width + 2
    )
    parts = halo_band(parts, 1, 5)
    band = band_cols + 2
    means = parts[..., out_width]
    mean = jnp.mean(means, axis=1)
    offsets = means - mean[:, None]
    m2 = jnp.sum(parts[..., out_width + 1], axis=1) + local_width * jnp.sum(
        offsets * offsets, axis=1
    )
    token_var = m2 / full_width
    centred_proj = jnp.sum(parts[..., :out_width], axis=1) + lax.dot_general(
        offsets,
        shard_columns,
        (((1,), (0,)), ((), ())),
        precision=lax.Precision.HIGHEST,
        preferred_element_type=jnp.float32,
    )
    velocity = lax.rsqrt(token_var + 1e-06)[..., None] * centred_proj + shift_column
    patches = (
        velocity.reshape(frames, window, band, LC, 2, 2)
        .transpose(0, 1, 4, 2, 5, 3)
        .reshape(frames, 2 * window, 2 * band, LC)
    )

    shares = neighbours(received[..., part_size:], sec, 0)
    if share == lines:
        shares = shares[:, :, 0]
    latent = shares.reshape(3, n_sp, frames, lat_cols, lat_rows, LC).transpose(0, 1, 2, 4, 3, 5)
    latent = halo_band(latent, 2, 4)
    if window == patch_rows:
        latent = latent.transpose(1, 0, 2, 3, 4).reshape(
            frames, n_sp * lat_rows, lat_cols + 4, LC
        )
        clean = latent - 0.5 * patches
        clean = jnp.pad(clean, ((0, 0), (2, 2), (0, 0), (0, 0)))
        clean = lax.dynamic_slice_in_dim(clean, spi * lat_rows, lat_rows + 4, 1)
    else:
        latent = neighbours(latent, spi, 0)
        latent = latent.transpose(1, 0, 2, 3, 4).reshape(
            frames, 3 * lat_rows, lat_cols + 4, LC
        )[:, lat_rows - 2 : 2 * lat_rows + 2]
        clean = latent - 0.5 * patches

    row_global = spi * lat_rows - 2 + jnp.arange(lat_rows + 4)
    col_global = sec * lat_cols - 2 + jnp.arange(lat_cols + 4)
    row_inside = (row_global >= 0) & (row_global < lat_rows * n_sp)
    col_inside = (col_global >= 0) & (col_global < lat_cols * n_sec)
    clean = jnp.where(row_inside[None, :, None, None] & col_inside[None, None, :, None], clean, 0.0)

    inner_features = valid_conv(causal_front(clean), in_weight, "DHWIO", lax.Precision.HIGH) + in_bias
    inside = row_inside[None, 1:-1, None, None] & col_inside[None, None, 1:-1, None]
    features = causal_front(jnp.where(inside, inner_features, 0.0).astype(jnp.bfloat16))
    upsampled = jnp.repeat(jnp.repeat(features, 2, axis=1), 2, axis=2)[:, 1:-1, 1:-1, :]
    mixed = valid_conv(upsampled, conv_weight, "DHWOI", None) + conv_bias

    group_size = CO // GROUPS
    local_groups = mixed.shape[-1] // group_size
    grouped = mixed.reshape(-1, local_groups, group_size)
    block_count = grouped.shape[0] * group_size
    block_mean = jnp.sum(grouped, axis=(0, 2)) / block_count
    deviation = grouped - block_mean[None, :, None]
    block_m2 = jnp.sum(deviation * deviation, axis=(0, 2))
    n_blocks = n_sec * n_sp
    stats = jnp.broadcast_to(
        jnp.concatenate([block_mean, block_m2])[None], (n_blocks, 2 * local_groups)
    )
    stats = lax.all_to_all(stats, BLOCKS, 0, 0, tiled=False)
    group_mean = jnp.mean(stats[:, :local_groups], axis=0)
    mean_offsets = stats[:, :local_groups] - group_mean[None]
    group_var = (
        jnp.sum(stats[:, local_groups:], axis=0)
        + block_count * jnp.sum(mean_offsets * mean_offsets, axis=0)
    ) / (block_count * n_blocks)

    normed = (
        (grouped - group_mean[None, :, None]) * lax.rsqrt(group_var + 1e-06)[None, :, None]
    ).reshape(mixed.shape)
    activated = jax.nn.silu(normed * norm_gain + norm_bias)
    out_rows, out_cols, out_chan = (activated.shape[1], activated.shape[2], activated.shape[3])
    return activated.transpose(1, 2, 3, 0).reshape(out_rows, out_cols, out_chan * frames)


def solution(mesh):
    return jax.shard_map(
        per_device,
        mesh=mesh,
        in_specs=(
            P("sp", None, "section", "rep"),
            P(),
            P(),
            P(),
            P(),
            P(None, "sp", "section", None),
            P(),
            P(),
            P(None, None, None, "rep", None),
            P("rep"),
            P("rep"),
            P("rep"),
        ),
        out_specs=P("sp", "section", "rep"),
        check_vma=False,
    )
```

```python
import jax
import jax.numpy as jnp
from jax import lax
from jax.experimental import pallas as pl
from jax.experimental.pallas import tpu as pltpu
from jax.sharding import PartitionSpec as P

D = 3072
LC = 16
CO = 256
GROUPS = 32
ALL = ("section", "sp", "rep")
BLOCKS = ("section", "sp")


def causal_front(volume):
    return jnp.concatenate([volume[:1], volume[:1], volume], axis=0)


def valid_conv(front, kernel, kernel_spec, precision_mode):
    result = lax.conv_general_dilated(
        front[None],
        kernel,
        (1, 1, 1),
        "VALID",
        dimension_numbers=("NDHWC", kernel_spec, "NDHWC"),
        precision=precision_mode,
        preferred_element_type=jnp.float32,
    )
    return result[0]


def shard_kernel(rep_ref, tok_ref, weight_ref, scale_ref, latent_ref, copies_ref):
    out_ref = copies_ref.at[0]
    weight = weight_ref[...] * (1.0 + scale_ref[...])
    width = weight.shape[0]
    band_cols = tok_ref.shape[1]
    record = width + 2
    for frame in range(tok_ref.shape[0]):
        for row in range(tok_ref.shape[2]):
            x = tok_ref[frame, :, row, :]
            mean = jnp.mean(x, axis=1, keepdims=True)
            centred = x - mean
            m2 = jnp.sum(centred * centred, axis=1, keepdims=True)
            projected = lax.dot_general(
                centred,
                weight,
                (((1,), (1,)), ((), ())),
                precision=lax.Precision.HIGHEST,
                preferred_element_type=jnp.float32,
            )
            for col in range(band_cols):
                base = ((frame * tok_ref.shape[2] + row) * band_cols + col) * record
                out_ref[:, pl.ds(base, width)] = projected[col : col + 1, :]
                out_ref[:, pl.ds(base + width, 1)] = mean[col : col + 1, :]
                out_ref[:, pl.ds(base + width + 1, 1)] = m2[col : col + 1, :]
    lines, lat_rows, channels = latent_ref.shape
    offset = tok_ref.shape[0] * tok_ref.shape[2] * band_cols * record
    share = latent_ref[...]
    for line in range(lines):
        for row in range(lat_rows):
            out_ref[:, pl.ds(offset + (line * lat_rows + row) * channels, channels)] = share[
                line, row : row + 1, :
            ]
    row_value = out_ref[...]
    for copy in range(1, copies_ref.shape[0]):
        copies_ref[copy] = row_value


def shard_moments(tokens, proj_weight, mod_scale, latent_lines, share, rep, copies):
    tok_frames, patch_rows, band_cols, local_width = tokens.shape
    out_width = proj_weight.shape[0]
    size = tok_frames * patch_rows * band_cols * (out_width + 2) + latent_lines[0].size * share
    whole = lambda i, r: (0, 0, 0, 0)
    whole3 = lambda i, r: (0, 0, 0)
    return pl.pallas_call(
        shard_kernel,
        grid_spec=pltpu.PrefetchScalarGridSpec(
            num_scalar_prefetch=1,
            grid=(1,),
            in_specs=[
                pl.BlockSpec((tok_frames, band_cols, patch_rows, local_width), whole),
                pl.BlockSpec((out_width, local_width), lambda i, r: (0, r[0])),
                pl.BlockSpec((1, local_width), lambda i, r: (0, r[0])),
                pl.BlockSpec(
                    (share,) + latent_lines.shape[1:],
                    (lambda i, r: (r[0], 0, 0)) if share < latent_lines.shape[0] else whole3,
                ),
            ],
            out_specs=pl.BlockSpec((copies, 1, size), whole3),
        ),
        out_shape=jax.ShapeDtypeStruct((copies, 1, size), jnp.float32),
    )(
        rep.reshape(1).astype(jnp.int32),
        tokens.transpose(0, 2, 1, 3),
        proj_weight,
        mod_scale.reshape(1, -1),
        latent_lines,
    )


def clamped_neighbours(stack, index):
    return jnp.stack(
        [lax.dynamic_index_in_dim(stack, index + d, 0, keepdims=False) for d in (-1, 0, 1)]
    )


def neighbours(stack, index, axis):
    pad = [(0, 0)] * stack.ndim
    pad[axis] = (1, 1)
    return lax.dynamic_slice_in_dim(jnp.pad(stack, pad), index, 3, axis)


def per_device(
    tokens,
    mod_scale,
    mod_shift,
    proj_weight,
    proj_bias,
    noisy_latent,
    in_weight,
    in_bias,
    conv_weight,
    conv_bias,
    norm_gain,
    norm_bias,
):
    n_sec, n_sp, n_rep = (lax.axis_size(a) for a in ALL)
    n_dev = n_sec * n_sp * n_rep
    sec, spi, rep = (lax.axis_index(a) for a in ALL)
    tok_frames, patch_rows, band_cols, local_width = tokens.shape
    frames, lat_rows, lat_cols, _ = noisy_latent.shape
    full_width = local_width * n_rep
    out_width = proj_weight.shape[0]


    lines = frames * lat_cols
    stored = noisy_latent.transpose(0, 2, 1, 3).reshape(lines, lat_rows, LC)
    share = lines // n_rep if lines % n_rep == 0 else lines
    slab = lat_rows // 2
    every_row = patch_rows <= slab + 2
    payload = shard_moments(
        tokens, proj_weight, mod_scale, stored, share, rep, n_dev if every_row else 1
    )
    part_flat = tok_frames * patch_rows * band_cols * (out_width + 2)

    if every_row:
        window = patch_rows
        part_size = part_flat
        send = payload
    else:
        payload = payload[0, 0]
        window = slab + 2
        partial = payload[:part_flat].reshape(tok_frames, patch_rows, band_cols, out_width + 2)
        padded = jnp.pad(partial, ((0, 0), (1, 1), (0, 0), (0, 0)))
        per_slab = jnp.stack([padded[:, p * slab : p * slab + window] for p in range(n_sp)])
        per_slab = per_slab.reshape(n_sp, -1)
        part_size = per_slab.shape[1]
        latent_part = payload[part_flat:]
        send = jnp.concatenate(
            [
                jnp.broadcast_to(per_slab[None, :, None], (n_sec, n_sp, n_rep, part_size)),
                jnp.broadcast_to(latent_part, (n_sec, n_sp, n_rep, latent_part.shape[0])),
            ],
            axis=-1,
        ).reshape(n_dev, -1)
    received = lax.all_to_all(send, ALL, 0, 0, tiled=False).reshape(n_sec, n_sp, n_rep, -1)

    scaled_weight = proj_weight * (1.0 + mod_scale)[None, :]
    shard_columns = jnp.sum(scaled_weight.reshape(out_width, n_rep, local_width), axis=2).T
    shift_column = (
        jnp.dot(
            proj_weight,
            mod_shift,
            precision=lax.Precision.HIGHEST,
            preferred_element_type=jnp.float32,
        )
        + proj_bias
    )
    def halo_band(stack, width, axis):
        return jnp.concatenate(
            [
                lax.slice_in_dim(stack[0], stack.shape[axis] - width, None, axis=axis - 1),
                stack[1],
                lax.slice_in_dim(stack[2], 0, width, axis=axis - 1),
            ],
            axis=axis - 1,
        )

    parts = clamped_neighbours(received[..., :part_size], sec).reshape(
        3, n_sp, n_rep, tok_frames, window, band_cols, out_width + 2
    )
    parts = halo_band(parts, 1, 5)
    band = band_cols + 2
    means = parts[..., out_width]
    mean = jnp.mean(means, axis=1)
    offsets = means - mean[:, None]
    m2 = jnp.sum(parts[..., out_width + 1], axis=1) + local_width * jnp.sum(
        offsets * offsets, axis=1
    )
    token_var = m2 / full_width
    centred_proj = jnp.sum(parts[..., :out_width], axis=1) + lax.dot_general(
        offsets,
        shard_columns,
        (((1,), (0,)), ((), ())),
        precision=lax.Precision.HIGHEST,
        preferred_element_type=jnp.float32,
    )
    velocity = lax.rsqrt(token_var + 1e-06)[..., None] * centred_proj + shift_column
    patches = (
        velocity.reshape(frames, window, band, LC, 2, 2)
        .transpose(0, 1, 4, 2, 5, 3)
        .reshape(frames, 2 * window, 2 * band, LC)
    )

    shares = clamped_neighbours(received[..., part_size:], sec)
    if share == lines:
        shares = shares[:, :, 0]
    latent = shares.reshape(3, n_sp, frames, lat_cols, lat_rows, LC).transpose(0, 1, 2, 4, 3, 5)
    latent = halo_band(latent, 2, 4)
    if window == patch_rows:
        latent = latent.transpose(1, 0, 2, 3, 4).reshape(
            frames, n_sp * lat_rows, lat_cols + 4, LC
        )
        clean = latent - 0.5 * patches
        clean = jnp.pad(clean, ((0, 0), (2, 2), (0, 0), (0, 0)))
        clean = lax.dynamic_slice_in_dim(clean, spi * lat_rows, lat_rows + 4, 1)
    else:
        latent = neighbours(latent, spi, 0)
        latent = latent.transpose(1, 0, 2, 3, 4).reshape(
            frames, 3 * lat_rows, lat_cols + 4, LC
        )[:, lat_rows - 2 : 2 * lat_rows + 2]
        clean = latent - 0.5 * patches

    row_global = spi * lat_rows - 2 + jnp.arange(lat_rows + 4)
    col_global = sec * lat_cols - 2 + jnp.arange(lat_cols + 4)
    row_inside = (row_global >= 0) & (row_global < lat_rows * n_sp)
    col_inside = (col_global >= 0) & (col_global < lat_cols * n_sec)
    clean = jnp.where(row_inside[None, :, None, None] & col_inside[None, None, :, None], clean, 0.0)

    inner_features = valid_conv(causal_front(clean), in_weight, "DHWIO", lax.Precision.HIGH) + in_bias
    inside = row_inside[None, 1:-1, None, None] & col_inside[None, None, 1:-1, None]
    features = causal_front(jnp.where(inside, inner_features, 0.0).astype(jnp.bfloat16))
    upsampled = jnp.repeat(jnp.repeat(features, 2, axis=1), 2, axis=2)[:, 1:-1, 1:-1, :]
    mixed = valid_conv(upsampled, conv_weight, "DHWOI", None) + conv_bias

    group_size = CO // GROUPS
    local_groups = mixed.shape[-1] // group_size
    grouped = mixed.reshape(-1, local_groups, group_size)
    block_count = grouped.shape[0] * group_size
    block_mean = jnp.sum(grouped, axis=(0, 2)) / block_count
    deviation = grouped - block_mean[None, :, None]
    block_m2 = jnp.sum(deviation * deviation, axis=(0, 2))
    n_blocks = n_sec * n_sp
    stats = jnp.broadcast_to(
        jnp.concatenate([block_mean, block_m2])[None], (n_blocks, 2 * local_groups)
    )
    stats = lax.all_to_all(stats, BLOCKS, 0, 0, tiled=False)
    group_mean = jnp.mean(stats[:, :local_groups], axis=0)
    mean_offsets = stats[:, :local_groups] - group_mean[None]
    group_var = (
        jnp.sum(stats[:, local_groups:], axis=0)
        + block_count * jnp.sum(mean_offsets * mean_offsets, axis=0)
    ) / (block_count * n_blocks)

    normed = (
        (grouped - group_mean[None, :, None]) * lax.rsqrt(group_var + 1e-06)[None, :, None]
    ).reshape(mixed.shape)
    activated = jax.nn.silu(normed * norm_gain + norm_bias)
    out_rows, out_cols, out_chan = (activated.shape[1], activated.shape[2], activated.shape[3])
    return activated.transpose(1, 2, 3, 0).reshape(out_rows, out_cols, out_chan * frames)


def solution(mesh):
    return jax.shard_map(
        per_device,
        mesh=mesh,
        in_specs=(
            P("sp", None, "section", "rep"),
            P(),
            P(),
            P(),
            P(),
            P(None, "sp", "section", None),
            P(),
            P(),
            P(None, None, None, "rep", None),
            P("rep"),
            P("rep"),
            P("rep"),
        ),
        out_specs=P("sp", "section", "rep"),
        check_vma=False,
    )
```
